256 devices in a mesh: ang: 128 (over z, x_lo, y, core), sl: 2 (over x_hi).
Axes of the slice: x: 4 (x_hi: 2, x_lo: 2; x = x_hi * 2 + x_lo), y: 4, z: 8, core: 2. Of those that a mesh axis runs over, the one named last changes fastest.
Arguments:
- projections: float32 [256, 8, 4352], P('ang', 'sl'), may hold values from -6 to 6
- partner: int32 [256], replicated, may hold values from 0 to 255, as said below
- offsets: int32 [256], P('ang'), may hold values from 0 to 192
- angles: float32 [256], replicated, may hold values from 0 to 6.2832, as said below
- coefficients: float32 [2, 8, 4096, 1280], P(None, None, ('ang', 'sl')), may hold values from -6 to 6
Outputs:
- updated: float32 [2, 8, 4096, 1280], P(None, None, ('ang', 'sl'))
- misfit: float32 [256, 8], P('ang', 'sl')
The draws below stay inside these ranges and needn't reach their ends.
Inputs may be any that keep to these rules, and one draw needn't show every extreme that they name: partner[partner[g]] = g, and g // 2 and partner[g] // 2 differ by 64: a projection's partner lies on the index of ang half the axis away. angles[partner[g]] lies within pi / 128 of angles[g] + pi or angles[g] - pi.
All inputs are finite; a program needn't handle non-finite values.
Results may differ from the reference program's by a relative error of at most 0.0003.
Values sent between devices are 32-bit elements; how exact they have to be, the bound alone decides.
No kernel may reach another device: no remote copies, remote signals or barrier semaphores. Data moves between devices by JAX's collectives and lax.ppermute only.
A program may use at most 64 MiB of HBM per device.

```python
import math
import jax
import jax.numpy as jnp
from jax import lax

W = 8192
HALF = 4096
K = 4096
EXTRA = 256
RAMP = 64
WH = 4352
ROWS = 8
M = 1280
A_DEV = 2
NANG = 256


def partner_table(key):
    half_devs = NANG // A_DEV // 2
    device_keys = jax.random.split(jax.random.fold_in(key, 101), half_devs)

    def one_order(sub_key):
        return jax.random.permutation(sub_key, A_DEV)
    orders = jax.vmap(one_order)(device_keys).astype(jnp.int32)
    inverse = jnp.argsort(orders, axis=1, stable=True).astype(jnp.int32)
    device_ids = jnp.arange(half_devs, dtype=jnp.int32)[:, None]
    first_half = (device_ids + half_devs) * A_DEV + orders
    second_half = device_ids * A_DEV + inverse
    return jnp.concatenate([first_half.reshape(-1), second_half.reshape(-1)]).astype(jnp.int32)


def draw_partner(key, part):
    return partner_table(key)


def draw_angles(key, part):
    pairs_table = partner_table(key)
    half_count = NANG // 2
    index_all = jnp.arange(NANG, dtype=jnp.int32)
    lower_half = index_all < half_count
    base_slot = jnp.where(lower_half, index_all, pairs_table).astype(jnp.float32)
    turn_base = jnp.where(lower_half, 0.0, math.pi).astype(jnp.float32)
    jitter = jax.random.uniform(jax.random.fold_in(key, 202), (NANG,), jnp.float32, 0.2, 0.8)
    return (turn_base + math.pi * (base_slot + jitter) / half_count).astype(jnp.float32)


def plant(entries, key, low, top_value):
    dims = entries.shape
    place = [jax.random.randint(jax.random.fold_in(key, axis), (), 0, dims[axis]) for axis in range(len(dims))]
    entries = entries.at[tuple(place)].set(low)
    longest = dims.index(max(dims))
    place[longest] = (place[longest] + 1) % dims[longest]
    return entries.at[tuple(place)].set(top_value)


def level_of(rng, extent, shards, smallest, high):
    loudness, own = 1.0, jax.random.fold_in(rng, 6)
    for axis_at, parts in shards:
        steps = jnp.exp(jax.random.uniform(jax.random.fold_in(own, axis_at), (parts,), jnp.float32, smallest / len(shards), high / len(shards)))
        loudness = loudness * jnp.repeat(steps, extent[axis_at] // parts).reshape([-1 if axis == axis_at else 1 for axis in range(len(extent))])
    return loudness


def gaussian(stream_key, extent, width, bound, shards=(), kind=jnp.bfloat16):
    gain = level_of(stream_key, extent, shards, -0.22, 0.18) if shards else 1.0
    values = jax.random.normal(stream_key, extent, jnp.float32) * width * gain
    return jnp.minimum(jnp.maximum(values, -bound), bound).astype(kind)


def setup_inputs(seed: int = 0) -> dict:
    seeds = jax.random.split(jax.random.key(seed), 6)
    projections = gaussian(seeds[0], (NANG, ROWS, WH), 1.0, 6.0, ((0, 128), (1, 2)), jnp.float32)
    partner = draw_partner(jax.random.fold_in(seeds[5], 71), 0)
    offsets = plant(jax.random.randint(seeds[2], (NANG,), 0, EXTRA - RAMP + 1), jax.random.fold_in(seeds[2], 1), 0, EXTRA - RAMP).astype(jnp.int32)
    angles = draw_angles(jax.random.fold_in(seeds[5], 71), 0)
    coefficients = gaussian(seeds[4], (2, ROWS, K, M), 1.0, 6.0, ((2, 256),), jnp.float32)
    return {"projections": projections, "partner": partner, "offsets": offsets, "angles": angles, "coefficients": coefficients}


paganin_strength = 16.0
small_eps = 1e-06
highest = lax.Precision.HIGHEST

def paganin_rows(frequencies):
    row_ids = jnp.arange(ROWS, dtype=jnp.int32)
    row_offset = (row_ids[:, None] - row_ids[None, :]) % ROWS
    cos_table = jnp.cos(2.0 * math.pi / ROWS * (row_ids[:, None, None] * row_offset[None, :, :] % ROWS).astype(jnp.float32))
    row_freq = jnp.minimum(row_ids, ROWS - row_ids).astype(jnp.float32) / ROWS
    col_freq = frequencies / W
    damping = 1.0 / (1.0 + paganin_strength * (col_freq[:, None] * col_freq[:, None] + row_freq[None, :] * row_freq[None, :]))
    return jnp.einsum('nq,qij->nij', damping, cos_table, precision=highest) / ROWS

def blend_band(projections, mirrored, offsets):
    position = jnp.arange(EXTRA, dtype=jnp.int32).astype(jnp.float32)
    weight = jnp.clip((position[None, :] - offsets[:, None].astype(jnp.float32)) / RAMP, 0.0, 1.0)
    own_band = projections[:, :, HALF - EXTRA:HALF]
    blended = own_band + weight[:, None, :] * (mirrored - own_band)
    return jnp.concatenate([projections[:, :, :HALF - EXTRA], blended], axis=2)

def apply_rows(harm_table, coef_part):
    return jnp.einsum('gm,cm->gc', harm_table, coef_part, precision=highest)

def apply_back(harm_table, resid_part):
    return jnp.einsum('gm,gc->cm', harm_table, resid_part, precision=highest)

def reference(projections, partner, offsets, angles, coefficients):
    total_angles = projections.shape[0]
    harmonics = coefficients.shape[3]
    mirrored = jnp.flip(jnp.take(projections[:, :, HALF:], partner, axis=0), axis=2)
    stitched = blend_band(projections, mirrored, offsets)
    spectrum = jnp.fft.rfft(stitched, n=W, axis=2)[:, :, :K] * (1.0 / math.sqrt(HALF))
    spec_real = jnp.real(spectrum)
    spec_imag = jnp.imag(spectrum)
    frequencies = jnp.arange(K, dtype=jnp.int32).astype(jnp.float32)
    turn_phase = 2.0 * math.pi / W * frequencies
    turn_cos = jnp.cos(turn_phase)
    turn_sin = jnp.sin(turn_phase)
    pair_real = jnp.take(spec_real, partner, axis=0)
    pair_imag = jnp.take(spec_imag, partner, axis=0)
    comb_real = spec_real + turn_cos * pair_real + turn_sin * pair_imag
    comb_imag = spec_imag + turn_sin * pair_real - turn_cos * pair_imag
    rows_matrix = paganin_rows(frequencies)
    filt_real = jnp.einsum('kij,gjk->gik', rows_matrix, comb_real, precision=highest)
    filt_imag = jnp.einsum('kij,gjk->gik', rows_matrix, comb_imag, precision=highest)
    weights_all = (frequencies + 0.5) / K
    harm_shift = (jnp.arange(harmonics, dtype=jnp.int32) - harmonics // 2).astype(jnp.float32)
    norm_scale = 1.0 / math.sqrt(harmonics)
    phase_tab = angles[:, None] * harm_shift[None, :]
    cos_tab = jnp.cos(phase_tab) * norm_scale
    sin_tab = jnp.sin(phase_tab) * norm_scale
    block_width = min(K, 256)
    block_count = K // block_width
    columns = ROWS * block_width

    def one_block(running, block_index):
        mis_acc, grad_acc, curv_acc = running
        start_at = block_index * block_width
        coef_blk = lax.dynamic_slice_in_dim(coefficients, start_at, block_width, 2).reshape(2, columns, harmonics)
        data_real = lax.dynamic_slice_in_dim(filt_real, start_at, block_width, 2).reshape(total_angles, columns)
        data_imag = lax.dynamic_slice_in_dim(filt_imag, start_at, block_width, 2).reshape(total_angles, columns)
        ramp_weights = jnp.tile(lax.dynamic_slice_in_dim(weights_all, start_at, block_width, 0), ROWS)
        model_real = apply_rows(cos_tab, coef_blk[0]) - apply_rows(sin_tab, coef_blk[1])
        model_imag = apply_rows(cos_tab, coef_blk[1]) + apply_rows(sin_tab, coef_blk[0])
        diff_real = model_real - data_real
        diff_imag = model_imag - data_imag
        resid_real = ramp_weights * diff_real
        resid_imag = ramp_weights * diff_imag
        energy = (diff_real * resid_real + diff_imag * resid_imag).reshape(total_angles, ROWS, block_width)
        mis_acc = mis_acc + lax.optimization_barrier(jnp.sum(energy, axis=2)) / K
        grad_real = apply_back(cos_tab, resid_real) + apply_back(sin_tab, resid_imag)
        grad_imag = apply_back(cos_tab, resid_imag) - apply_back(sin_tab, resid_real)
        image_real = apply_rows(cos_tab, grad_real) - apply_rows(sin_tab, grad_imag)
        image_imag = apply_rows(cos_tab, grad_imag) + apply_rows(sin_tab, grad_real)
        curv_acc = curv_acc + jnp.sum(ramp_weights * (image_real * image_real + image_imag * image_imag))
        grad_acc = grad_acc + jnp.sum(grad_real * grad_real + grad_imag * grad_imag)
        grad_block = jnp.stack([grad_real, grad_imag]).reshape(2, ROWS, block_width, harmonics)
        return ((mis_acc, grad_acc, curv_acc), grad_block)
    start_state = (jnp.zeros((total_angles, ROWS), jnp.float32), jnp.float32(0.0), jnp.float32(0.0))
    final_state, grad_blocks = lax.scan(one_block, start_state, jnp.arange(block_count, dtype=jnp.int32))
    misfit, grad_norm, curvature = final_state
    gradient = jnp.moveaxis(grad_blocks, 0, 2).reshape(2, ROWS, K, harmonics)
    step_size = grad_norm / (curvature + small_eps)
    return (coefficients - step_size * gradient, misfit)
```

```python
import functools
import math

import jax
import jax.numpy as jnp
from jax import lax
from jax.sharding import Mesh
from jax.sharding import PartitionSpec as P

W = 8192
HALF = 4096
K = 4096
EXTRA = 256
RAMP = 64
ROWS = 8
ANG = ("ang_0", "ang_1", "ang_2", "ang_3")
ANG_SL = ("ang_0", "ang_1", "ang_2", "ang_3", "sl")


paganin_strength = 16.0
small_eps = 1e-06
highest = lax.Precision.HIGHEST


def from_behind(value, axis, steps):
    count = lax.axis_size(axis)
    pairs = [(source, (source + steps) % count) for source in range(count)]
    return lax.ppermute(value, axis, pairs)


def in_blocks(value, dim, length):
    before, after = (value.shape[:dim], value.shape[dim + 1 :])
    return jnp.moveaxis(value.reshape(*before, length, -1, *after), dim, 0)


def laid_out(parts, dim):
    parts = jnp.moveaxis(parts, 0, dim)
    shape = parts.shape
    return parts.reshape(*shape[:dim], shape[dim] * shape[dim + 1], *shape[dim + 2 :])


def exchange_both(value, axis, axes, splits, concats):
    sizes = [lax.axis_size(a) for a in axes]
    parts = in_blocks(value, splits[0], sizes[0])
    parts = jnp.moveaxis(in_blocks(parts, splits[1] + 1, sizes[1]), 0, 1)
    inside = parts.shape[2:]
    parts = parts.reshape(-1, *inside)
    parts = lax.all_to_all(parts, axis, split_axis=0, concat_axis=0, tiled=True)
    parts = laid_out(parts.reshape(*sizes, *inside), concats[0] + 1)
    return laid_out(parts, concats[1])


def by_axis(value, axes):
    return functools.reduce(lax.psum, axes, value)


def paganin_rows(frequencies):
    row_ids = jnp.arange(ROWS, dtype=jnp.int32)
    row_offset = (row_ids[:, None] - row_ids[None, :]) % ROWS
    cos_table = jnp.cos(
        2.0
        * math.pi
        / ROWS
        * (row_ids[:, None, None] * row_offset[None, :, :] % ROWS).astype(jnp.float32)
    )
    row_freq = jnp.minimum(row_ids, ROWS - row_ids).astype(jnp.float32) / ROWS
    col_freq = frequencies / W
    damping = 1.0 / (
        1.0
        + paganin_strength
        * (col_freq[:, None] * col_freq[:, None] + row_freq[None, :] * row_freq[None, :])
    )
    return jnp.einsum("nq,qij->nij", damping, cos_table, precision=highest) / ROWS


def blend_band(projections, mirrored, offsets):
    position = jnp.arange(EXTRA, dtype=jnp.int32).astype(jnp.float32)
    weight = jnp.clip((position[None, :] - offsets[:, None].astype(jnp.float32)) / RAMP, 0.0, 1.0)
    own_band = projections[:, :, HALF - EXTRA : HALF]
    blended = own_band + weight[:, None, :] * (mirrored - own_band)
    return jnp.concatenate([projections[:, :, : HALF - EXTRA], blended], axis=2)


def spectrum_of(stitched):
    row_count = stitched.shape[0] * stitched.shape[1]
    low_split = W // 128
    outer_count = HALF // low_split
    high_count = K // 128
    folded = stitched.reshape(row_count, outer_count, low_split)
    norm_scale = 1.0 / math.sqrt(HALF)
    outer_ids = jnp.arange(outer_count, dtype=jnp.int32)
    lane_ids = jnp.arange(128, dtype=jnp.int32)
    first_phase = (
        2.0 * math.pi / 128 * (outer_ids[:, None] * lane_ids[None, :] % 128).astype(jnp.float32)
    )
    first_cos = jnp.cos(first_phase) * norm_scale
    first_sin = jnp.sin(first_phase) * norm_scale
    part_real = jnp.einsum("rab,ap->rbp", folded, first_cos, precision=highest)
    part_imag = -jnp.einsum("rab,ap->rbp", folded, first_sin, precision=highest)
    low_ids = jnp.arange(low_split, dtype=jnp.int32)
    twist_phase = 2.0 * math.pi / W * (low_ids[:, None] * lane_ids[None, :]).astype(jnp.float32)
    twist_cos = jnp.cos(twist_phase)
    twist_sin = jnp.sin(twist_phase)
    turned_real = part_real * twist_cos + part_imag * twist_sin
    turned_imag = part_imag * twist_cos - part_real * twist_sin
    high_ids = jnp.arange(high_count, dtype=jnp.int32)
    last_phase = (
        2.0
        * math.pi
        / low_split
        * (low_ids[:, None] * high_ids[None, :] % low_split).astype(jnp.float32)
    )
    last_cos = jnp.cos(last_phase)
    last_sin = jnp.sin(last_phase)
    spec_real = jnp.einsum("rbp,bq->rqp", turned_real, last_cos, precision=highest) + jnp.einsum(
        "rbp,bq->rqp", turned_imag, last_sin, precision=highest
    )
    spec_imag = jnp.einsum("rbp,bq->rqp", turned_imag, last_cos, precision=highest) - jnp.einsum(
        "rbp,bq->rqp", turned_real, last_sin, precision=highest
    )
    out_shape = (stitched.shape[0], stitched.shape[1], K)
    return (spec_real.reshape(out_shape), spec_imag.reshape(out_shape))


def apply_rows(harm_table, coef_part):
    return jnp.einsum("gm,cm->gc", harm_table, coef_part, precision=highest)


def apply_back(harm_table, resid_part):
    return jnp.einsum("gm,gc->cm", harm_table, resid_part, precision=highest)


def shards(projections, partner, offsets, angles, coefficients):
    ang_count = lax.axis_size(ANG)
    sl_count = lax.axis_size("sl")
    ang_index = lax.axis_index(ANG)
    sl_index = lax.axis_index("sl")
    per_dev = projections.shape[0]
    rows_dev = projections.shape[1]
    total_angles = per_dev * ang_count
    block_freqs = coefficients.shape[2]
    harmonics = coefficients.shape[3]
    columns = ROWS * block_freqs
    own_partners = lax.dynamic_slice_in_dim(partner, ang_index * per_dev, per_dev)
    across_dev = (ang_index + ang_count // 2) % ang_count
    partner_slots = own_partners - across_dev * per_dev
    arrived = from_behind(projections[:, :, HALF:], ANG, ang_count // 2)
    mirrored = jnp.flip(jnp.take(arrived, partner_slots, axis=0), axis=2)
    stitched = blend_band(projections, mirrored, offsets)
    spec_real, spec_imag = spectrum_of(stitched)
    spectra = jnp.stack([spec_real, spec_imag])
    regrouped = exchange_both(spectra, ANG_SL, (ANG, "sl"), (3, 3), (1, 2))
    freq_major = regrouped.reshape(2, total_angles, columns)
    freq_base = (ang_index * sl_count + sl_index) * block_freqs
    local_freq = (freq_base + jnp.arange(block_freqs, dtype=jnp.int32)).astype(jnp.float32)
    col_freq = jnp.tile(local_freq, ROWS)
    turn_phase = 2.0 * math.pi / W * col_freq
    turn_cos = jnp.cos(turn_phase)
    turn_sin = jnp.sin(turn_phase)
    own_real = freq_major[0]
    own_imag = freq_major[1]
    pair_real = jnp.take(own_real, partner, axis=0)
    pair_imag = jnp.take(own_imag, partner, axis=0)
    comb_real = own_real + turn_cos * pair_real + turn_sin * pair_imag
    comb_imag = own_imag + turn_sin * pair_real - turn_cos * pair_imag
    rows_matrix = paganin_rows(local_freq)
    full_matrix = jnp.einsum(
        "nij,mn->jmin", rows_matrix, jnp.eye(block_freqs, dtype=jnp.float32)
    ).reshape(columns, columns)
    filt_real = jnp.dot(comb_real, full_matrix, precision=highest)
    filt_imag = jnp.dot(comb_imag, full_matrix, precision=highest)
    ramp_weights = (col_freq + 0.5) / K
    coef_rows = coefficients.reshape(2 * columns, harmonics)
    harm_shift = (jnp.arange(harmonics, dtype=jnp.int32) - harmonics // 2).astype(jnp.float32)
    norm_scale = 1.0 / math.sqrt(harmonics)
    phase_tab = angles[:, None] * harm_shift[None, :]
    tabs = jnp.concatenate([jnp.cos(phase_tab) * norm_scale, jnp.sin(phase_tab) * norm_scale])

    def to_image(coef):
        prod = lax.dot_general(
            tabs, coef, (((1,), (1,)), ((), ())), precision=highest
        )
        cos_part, sin_part = prod[:total_angles], prod[total_angles:]
        real = cos_part[:, :columns] - sin_part[:, columns:]
        imag = cos_part[:, columns:] + sin_part[:, :columns]
        return real, imag

    model_real, model_imag = to_image(coef_rows)
    diff_real = model_real - filt_real
    diff_imag = model_imag - filt_imag
    resid_real = ramp_weights * diff_real
    resid_imag = ramp_weights * diff_imag
    energy = (diff_real * resid_real + diff_imag * resid_imag).reshape(
        total_angles, ROWS, block_freqs
    )
    misfit_table = jnp.sum(energy, axis=2) / K
    stacked = jnp.concatenate(
        [
            jnp.concatenate([resid_real, resid_imag], axis=1),
            jnp.concatenate([resid_imag, -resid_real], axis=1),
        ]
    )
    grad = lax.dot_general(stacked, tabs, (((0,), (0,)), ((), ())), precision=highest)
    image_real, image_imag = to_image(grad)
    curvature = jnp.sum(ramp_weights * (image_real * image_real + image_imag * image_imag))
    grad_norm = jnp.sum(grad * grad)
    table_total = lax.psum(misfit_table, ANG_SL)
    sums = lax.psum(jnp.stack([grad_norm, curvature]), ANG_SL)
    misfit = lax.dynamic_slice(
        table_total, (ang_index * per_dev, sl_index * rows_dev), (per_dev, rows_dev)
    )
    step_size = sums[0] / (sums[1] + small_eps)
    updated = coefficients - step_size * grad.reshape(coefficients.shape)
    return (updated, misfit)


def solution(mesh):
    torus = Mesh(
        mesh.devices.reshape(8, 2, 4, 2, mesh.shape["sl"]),
        ("ang_0", "ang_1", "ang_2", "ang_3", "sl"),
    )
    in_specs = (P(ANG, "sl", None), P(), P(ANG), P(), P(None, None, ANG_SL, None))
    out_specs = (P(None, None, ANG_SL, None), P(ANG, "sl"))
    return jax.shard_map(
        shards, mesh=torus, in_specs=in_specs, out_specs=out_specs, check_vma=False
    )
```

```python
import functools
import math

import jax
import jax.numpy as jnp
from jax import lax
from jax.sharding import Mesh
from jax.sharding import PartitionSpec as P

W = 8192
HALF = 4096
K = 4096
EXTRA = 256
RAMP = 64
ROWS = 8
ANG = ("ang_0", "ang_1", "ang_2", "ang_3")
ANG_SL = ("ang_0", "ang_1", "ang_2", "ang_3", "sl")


paganin_strength = 16.0
small_eps = 1e-06
highest = lax.Precision.HIGHEST


def from_behind(value, axis, steps):
    count = lax.axis_size(axis)
    pairs = [(source, (source + steps) % count) for source in range(count)]
    return lax.ppermute(value, axis, pairs)


def in_blocks(value, dim, length):
    before, after = (value.shape[:dim], value.shape[dim + 1 :])
    return jnp.moveaxis(value.reshape(*before, length, -1, *after), dim, 0)


def laid_out(parts, dim):
    parts = jnp.moveaxis(parts, 0, dim)
    shape = parts.shape
    return parts.reshape(*shape[:dim], shape[dim] * shape[dim + 1], *shape[dim + 2 :])


def exchange_both(value, axis, axes, splits, concats):
    sizes = [lax.axis_size(a) for a in axes]
    parts = in_blocks(value, splits[0], sizes[0])
    parts = jnp.moveaxis(in_blocks(parts, splits[1] + 1, sizes[1]), 0, 1)
    inside = parts.shape[2:]
    parts = parts.reshape(-1, *inside)
    parts = lax.all_to_all(parts, axis, split_axis=0, concat_axis=0, tiled=True)
    parts = laid_out(parts.reshape(*sizes, *inside), concats[0] + 1)
    return laid_out(parts, concats[1])


def by_axis(value, axes):
    return functools.reduce(lax.psum, axes, value)


def paganin_rows(frequencies):
    row_ids = jnp.arange(ROWS, dtype=jnp.int32)
    row_offset = (row_ids[:, None] - row_ids[None, :]) % ROWS
    cos_table = jnp.cos(
        2.0
        * math.pi
        / ROWS
        * (row_ids[:, None, None] * row_offset[None, :, :] % ROWS).astype(jnp.float32)
    )
    row_freq = jnp.minimum(row_ids, ROWS - row_ids).astype(jnp.float32) / ROWS
    col_freq = frequencies / W
    damping = 1.0 / (
        1.0
        + paganin_strength
        * (col_freq[:, None] * col_freq[:, None] + row_freq[None, :] * row_freq[None, :])
    )
    return jnp.einsum("nq,qij->nij", damping, cos_table, precision=highest) / ROWS


def blend_band(projections, mirrored, offsets):
    position = jnp.arange(EXTRA, dtype=jnp.int32).astype(jnp.float32)
    weight = jnp.clip((position[None, :] - offsets[:, None].astype(jnp.float32)) / RAMP, 0.0, 1.0)
    own_band = projections[:, :, HALF - EXTRA : HALF]
    blended = own_band + weight[:, None, :] * (mirrored - own_band)
    return jnp.concatenate([projections[:, :, : HALF - EXTRA], blended], axis=2)


def spectrum_of(stitched):
    row_count = stitched.shape[0] * stitched.shape[1]
    low_split = W // 128
    outer_count = HALF // low_split
    high_count = K // 128
    folded = stitched.reshape(row_count, outer_count, low_split)
    norm_scale = 1.0 / math.sqrt(HALF)
    outer_ids = jnp.arange(outer_count, dtype=jnp.int32)
    lane_ids = jnp.arange(128, dtype=jnp.int32)
    first_phase = (
        2.0 * math.pi / 128 * (outer_ids[:, None] * lane_ids[None, :] % 128).astype(jnp.float32)
    )
    first_cos = jnp.cos(first_phase) * norm_scale
    first_sin = jnp.sin(first_phase) * norm_scale
    part_real = jnp.einsum("rab,ap->rbp", folded, first_cos, precision=highest)
    part_imag = -jnp.einsum("rab,ap->rbp", folded, first_sin, precision=highest)
    low_ids = jnp.arange(low_split, dtype=jnp.int32)
    twist_phase = 2.0 * math.pi / W * (low_ids[:, None] * lane_ids[None, :]).astype(jnp.float32)
    twist_cos = jnp.cos(twist_phase)
    twist_sin = jnp.sin(twist_phase)
    turned_real = part_real * twist_cos + part_imag * twist_sin
    turned_imag = part_imag * twist_cos - part_real * twist_sin
    high_ids = jnp.arange(high_count, dtype=jnp.int32)
    last_phase = (
        2.0
        * math.pi
        / low_split
        * (low_ids[:, None] * high_ids[None, :] % low_split).astype(jnp.float32)
    )
    last_cos = jnp.cos(last_phase)
    last_sin = jnp.sin(last_phase)
    spec_real = jnp.einsum("rbp,bq->rqp", turned_real, last_cos, precision=highest) + jnp.einsum(
        "rbp,bq->rqp", turned_imag, last_sin, precision=highest
    )
    spec_imag = jnp.einsum("rbp,bq->rqp", turned_imag, last_cos, precision=highest) - jnp.einsum(
        "rbp,bq->rqp", turned_real, last_sin, precision=highest
    )
    out_shape = (stitched.shape[0], stitched.shape[1], K)
    return (spec_real.reshape(out_shape), spec_imag.reshape(out_shape))


def apply_rows(harm_table, coef_part):
    return jnp.einsum("gm,cm->gc", harm_table, coef_part, precision=highest)


def apply_back(harm_table, resid_part):
    return jnp.einsum("gm,gc->cm", harm_table, resid_part, precision=highest)


def shards(projections, partner, offsets, angles, coefficients):
    ang_count = lax.axis_size(ANG)
    sl_count = lax.axis_size("sl")
    ang_index = lax.axis_index(ANG)
    sl_index = lax.axis_index("sl")
    per_dev = projections.shape[0]
    rows_dev = projections.shape[1]
    total_angles = per_dev * ang_count
    block_freqs = coefficients.shape[2]
    harmonics = coefficients.shape[3]
    columns = ROWS * block_freqs
    own_partners = lax.dynamic_slice_in_dim(partner, ang_index * per_dev, per_dev)
    across_dev = (ang_index + ang_count // 2) % ang_count
    partner_slots = own_partners - across_dev * per_dev
    arrived = from_behind(projections[:, :, HALF:], ANG, ang_count // 2)
    mirrored = jnp.flip(jnp.take(arrived, partner_slots, axis=0), axis=2)
    stitched = blend_band(projections, mirrored, offsets)
    spec_real, spec_imag = spectrum_of(stitched)
    spectra = jnp.stack([spec_real, spec_imag])
    regrouped = exchange_both(spectra, ANG_SL, (ANG, "sl"), (3, 3), (1, 2))
    freq_major = regrouped.reshape(2, total_angles, columns)
    freq_base = (ang_index * sl_count + sl_index) * block_freqs
    local_freq = (freq_base + jnp.arange(block_freqs, dtype=jnp.int32)).astype(jnp.float32)
    col_freq = jnp.tile(local_freq, ROWS)
    turn_phase = 2.0 * math.pi / W * col_freq
    turn_cos = jnp.cos(turn_phase)
    turn_sin = jnp.sin(turn_phase)
    own_real = freq_major[0]
    own_imag = freq_major[1]
    pair_real = jnp.take(own_real, partner, axis=0)
    pair_imag = jnp.take(own_imag, partner, axis=0)
    comb_real = own_real + turn_cos * pair_real + turn_sin * pair_imag
    comb_imag = own_imag + turn_sin * pair_real - turn_cos * pair_imag
    rows_matrix = paganin_rows(local_freq)
    full_matrix = jnp.einsum(
        "nij,mn->jmin", rows_matrix, jnp.eye(block_freqs, dtype=jnp.float32)
    ).reshape(columns, columns)
    filt_real = jnp.dot(comb_real, full_matrix, precision=highest)
    filt_imag = jnp.dot(comb_imag, full_matrix, precision=highest)
    ramp_weights = (col_freq + 0.5) / K
    coef_rows = coefficients.reshape(2 * columns, harmonics)
    harm_shift = (jnp.arange(harmonics, dtype=jnp.int32) - harmonics // 2).astype(jnp.float32)
    norm_scale = 1.0 / math.sqrt(harmonics)
    phase_tab = angles[:, None] * harm_shift[None, :]
    tabs = jnp.concatenate([jnp.cos(phase_tab) * norm_scale, jnp.sin(phase_tab) * norm_scale])

    def to_image(coef):
        prod = lax.dot_general(
            tabs, coef, (((1,), (1,)), ((), ())), precision=highest
        )
        cos_part, sin_part = prod[:total_angles], prod[total_angles:]
        real = cos_part[:, :columns] - sin_part[:, columns:]
        imag = cos_part[:, columns:] + sin_part[:, :columns]
        return real, imag

    model_real, model_imag = to_image(coef_rows)
    diff_real = model_real - filt_real
    diff_imag = model_imag - filt_imag
    resid_real = ramp_weights * diff_real
    resid_imag = ramp_weights * diff_imag
    energy = (diff_real * resid_real + diff_imag * resid_imag).reshape(
        total_angles, ROWS, block_freqs
    )
    misfit_table = jnp.sum(energy, axis=2) / K
    stacked = jnp.concatenate(
        [
            jnp.concatenate([resid_real, resid_imag], axis=1),
            jnp.concatenate([resid_imag, -resid_real], axis=1),
        ]
    )
    grad = lax.dot_general(stacked, tabs, (((0,), (0,)), ((), ())), precision=highest)
    image_real, image_imag = to_image(grad)
    curvature = jnp.sum(ramp_weights * (image_real * image_real + image_imag * image_imag))
    grad_norm = jnp.sum(grad * grad)
    by_owner = misfit_table.reshape(ang_count, per_dev, sl_count, rows_dev)
    by_owner = jnp.swapaxes(by_owner, 1, 2).reshape(ang_count * sl_count, per_dev * rows_dev)
    scalars = jnp.broadcast_to(jnp.stack([grad_norm, curvature])[None], (ang_count * sl_count, 2))
    payload = jnp.concatenate([by_owner, scalars], axis=1)
    received = lax.all_to_all(payload, ANG_SL, 0, 0, tiled=True)
    totals = jnp.sum(received, axis=0)
    misfit = totals[: per_dev * rows_dev].reshape(per_dev, rows_dev)
    step_size = totals[per_dev * rows_dev] / (totals[per_dev * rows_dev + 1] + small_eps)
    updated = coefficients - step_size * grad.reshape(coefficients.shape)
    return (updated, misfit)


def solution(mesh):
    torus = Mesh(
        mesh.devices.reshape(8, 2, 4, 2, mesh.shape["sl"]),
        ("ang_0", "ang_1", "ang_2", "ang_3", "sl"),
    )
    in_specs = (P(ANG, "sl", None), P(), P(ANG), P(), P(None, None, ANG_SL, None))
    out_specs = (P(None, None, ANG_SL, None), P(ANG, "sl"))
    return jax.shard_map(
        shards, mesh=torus, in_specs=in_specs, out_specs=out_specs, check_vma=False
    )
```

```python
import functools
import math

import jax
import jax.numpy as jnp
from jax import lax
from jax.sharding import Mesh
from jax.sharding import PartitionSpec as P

W = 8192
HALF = 4096
K = 4096
EXTRA = 256
RAMP = 64
ROWS = 8
ANG = ("ang_0", "ang_1", "ang_2", "ang_3")
ANG_SL = ("ang_0", "ang_1", "ang_2", "ang_3", "sl")


paganin_strength = 16.0
small_eps = 1e-06
highest = lax.Precision.HIGHEST


def from_behind(value, axis, steps):
    count = lax.axis_size(axis)
    pairs = [(source, (source + steps) % count) for source in range(count)]
    return lax.ppermute(value, axis, pairs)


def in_blocks(value, dim, length):
    before, after = (value.shape[:dim], value.shape[dim + 1 :])
    return jnp.moveaxis(value.reshape(*before, length, -1, *after), dim, 0)


def laid_out(parts, dim):
    parts = jnp.moveaxis(parts, 0, dim)
    shape = parts.shape
    return parts.reshape(*shape[:dim], shape[dim] * shape[dim + 1], *shape[dim + 2 :])


def exchange_both(value, axis, axes, splits, concats):
    sizes = [lax.axis_size(a) for a in axes]
    parts = in_blocks(value, splits[0], sizes[0])
    parts = jnp.moveaxis(in_blocks(parts, splits[1] + 1, sizes[1]), 0, 1)
    inside = parts.shape[2:]
    parts = parts.reshape(-1, *inside)
    parts = lax.all_to_all(parts, axis, split_axis=0, concat_axis=0, tiled=True)
    parts = laid_out(parts.reshape(*sizes, *inside), concats[0] + 1)
    return laid_out(parts, concats[1])


def by_axis(value, axes):
    return functools.reduce(lax.psum, axes, value)


def paganin_rows(frequencies):
    row_ids = jnp.arange(ROWS, dtype=jnp.int32)
    row_offset = (row_ids[:, None] - row_ids[None, :]) % ROWS
    cos_table = jnp.cos(
        2.0
        * math.pi
        / ROWS
        * (row_ids[:, None, None] * row_offset[None, :, :] % ROWS).astype(jnp.float32)
    )
    row_freq = jnp.minimum(row_ids, ROWS - row_ids).astype(jnp.float32) / ROWS
    col_freq = frequencies / W
    damping = 1.0 / (
        1.0
        + paganin_strength
        * (col_freq[:, None] * col_freq[:, None] + row_freq[None, :] * row_freq[None, :])
    )
    return jnp.einsum("nq,qij->nij", damping, cos_table, precision=highest) / ROWS


def blend_band(projections, mirrored, offsets):
    position = jnp.arange(EXTRA, dtype=jnp.int32).astype(jnp.float32)
    weight = jnp.clip((position[None, :] - offsets[:, None].astype(jnp.float32)) / RAMP, 0.0, 1.0)
    own_band = projections[:, :, HALF - EXTRA : HALF]
    blended = own_band + weight[:, None, :] * (mirrored - own_band)
    return jnp.concatenate([projections[:, :, : HALF - EXTRA], blended], axis=2)


def spectrum_of(stitched):
    row_count = stitched.shape[0] * stitched.shape[1]
    low_split = W // 128
    outer_count = HALF // low_split
    high_count = K // 128
    folded = stitched.reshape(row_count, outer_count, low_split)
    norm_scale = 1.0 / math.sqrt(HALF)
    outer_ids = jnp.arange(outer_count, dtype=jnp.int32)
    lane_ids = jnp.arange(128, dtype=jnp.int32)
    first_phase = (
        2.0 * math.pi / 128 * (outer_ids[:, None] * lane_ids[None, :] % 128).astype(jnp.float32)
    )
    first_cos = jnp.cos(first_phase) * norm_scale
    first_sin = jnp.sin(first_phase) * norm_scale
    part_real = jnp.einsum("rab,ap->rbp", folded, first_cos, precision=highest)
    part_imag = -jnp.einsum("rab,ap->rbp", folded, first_sin, precision=highest)
    low_ids = jnp.arange(low_split, dtype=jnp.int32)
    twist_phase = 2.0 * math.pi / W * (low_ids[:, None] * lane_ids[None, :]).astype(jnp.float32)
    twist_cos = jnp.cos(twist_phase)
    twist_sin = jnp.sin(twist_phase)
    turned_real = part_real * twist_cos + part_imag * twist_sin
    turned_imag = part_imag * twist_cos - part_real * twist_sin
    high_ids = jnp.arange(high_count, dtype=jnp.int32)
    last_phase = (
        2.0
        * math.pi
        / low_split
        * (low_ids[:, None] * high_ids[None, :] % low_split).astype(jnp.float32)
    )
    last_cos = jnp.cos(last_phase)
    last_sin = jnp.sin(last_phase)
    spec_real = jnp.einsum("rbp,bq->rqp", turned_real, last_cos, precision=highest) + jnp.einsum(
        "rbp,bq->rqp", turned_imag, last_sin, precision=highest
    )
    spec_imag = jnp.einsum("rbp,bq->rqp", turned_imag, last_cos, precision=highest) - jnp.einsum(
        "rbp,bq->rqp", turned_real, last_sin, precision=highest
    )
    return (spec_real, spec_imag)


def apply_rows(harm_table, coef_part):
    return jnp.einsum("gm,cm->gc", harm_table, coef_part, precision=highest)


def apply_back(harm_table, resid_part):
    return jnp.einsum("gm,gc->cm", harm_table, resid_part, precision=highest)


def shards(projections, partner, offsets, angles, coefficients):
    ang_count = lax.axis_size(ANG)
    sl_count = lax.axis_size("sl")
    ang_index = lax.axis_index(ANG)
    sl_index = lax.axis_index("sl")
    per_dev = projections.shape[0]
    rows_dev = projections.shape[1]
    total_angles = per_dev * ang_count
    block_freqs = coefficients.shape[2]
    harmonics = coefficients.shape[3]
    columns = ROWS * block_freqs
    own_partners = lax.dynamic_slice_in_dim(partner, ang_index * per_dev, per_dev)
    across_dev = (ang_index + ang_count // 2) % ang_count
    partner_slots = own_partners - across_dev * per_dev
    arrived = from_behind(projections[:, :, HALF:], ANG, ang_count // 2)
    mirrored = jnp.flip(jnp.take(arrived, partner_slots, axis=0), axis=2)
    stitched = blend_band(projections, mirrored, offsets)
    spec_real, spec_imag = spectrum_of(stitched)
    spectra = jnp.stack([spec_real, spec_imag])
    dev_count = ang_count * sl_count
    lane_split = 128 // block_freqs
    spectra = spectra.reshape(2, per_dev * rows_dev, K // 128, lane_split, block_freqs)
    payload = spectra.transpose(2, 3, 0, 1, 4).reshape(dev_count, -1)
    received = lax.all_to_all(payload, ANG_SL, 0, 0, tiled=True)
    received = received.reshape(ang_count, sl_count, 2, per_dev, rows_dev * block_freqs)
    freq_major = received.transpose(2, 0, 3, 1, 4).reshape(2, total_angles, columns)
    freq_base = (ang_index * sl_count + sl_index) * block_freqs
    local_freq = (freq_base + jnp.arange(block_freqs, dtype=jnp.int32)).astype(jnp.float32)
    col_freq = jnp.tile(local_freq, ROWS)
    turn_phase = 2.0 * math.pi / W * col_freq
    turn_cos = jnp.cos(turn_phase)
    turn_sin = jnp.sin(turn_phase)
    own_real = freq_major[0]
    own_imag = freq_major[1]
    swap = (partner[:, None] == jnp.arange(total_angles, dtype=jnp.int32)[None, :]).astype(jnp.float32)
    own_both = jnp.concatenate([own_real, own_imag], axis=1)
    pair_both = jnp.dot(swap, own_both, precision=highest)
    pair_real = pair_both[:, :columns]
    pair_imag = pair_both[:, columns:]
    comb_real = own_real + turn_cos * pair_real + turn_sin * pair_imag
    comb_imag = own_imag + turn_sin * pair_real - turn_cos * pair_imag
    rows_matrix = paganin_rows(local_freq)
    full_matrix = jnp.einsum(
        "nij,mn->jmin", rows_matrix, jnp.eye(block_freqs, dtype=jnp.float32)
    ).reshape(columns, columns)
    filt_real = jnp.dot(comb_real, full_matrix, precision=highest)
    filt_imag = jnp.dot(comb_imag, full_matrix, precision=highest)
    ramp_weights = (col_freq + 0.5) / K
    coef_rows = coefficients.reshape(2 * columns, harmonics)
    harm_shift = (jnp.arange(harmonics, dtype=jnp.int32) - harmonics // 2).astype(jnp.float32)
    norm_scale = 1.0 / math.sqrt(harmonics)
    phase_tab = angles[:, None] * harm_shift[None, :]
    tabs = jnp.concatenate([jnp.cos(phase_tab) * norm_scale, jnp.sin(phase_tab) * norm_scale])

    def to_image(coef):
        prod = lax.dot_general(
            tabs, coef, (((1,), (1,)), ((), ())), precision=highest
        )
        cos_part, sin_part = prod[:total_angles], prod[total_angles:]
        real = cos_part[:, :columns] - sin_part[:, columns:]
        imag = cos_part[:, columns:] + sin_part[:, :columns]
        return real, imag

    model_real, model_imag = to_image(coef_rows)
    diff_real = model_real - filt_real
    diff_imag = model_imag - filt_imag
    resid_real = ramp_weights * diff_real
    resid_imag = ramp_weights * diff_imag
    energy = (diff_real * resid_real + diff_imag * resid_imag).reshape(
        total_angles, ROWS, block_freqs
    )
    misfit_table = jnp.sum(energy, axis=2) / K
    stacked = jnp.concatenate(
        [
            jnp.concatenate([resid_real, resid_imag], axis=1),
            jnp.concatenate([resid_imag, -resid_real], axis=1),
        ]
    )
    grad = lax.dot_general(stacked, tabs, (((0,), (0,)), ((), ())), precision=highest)
    image_real, image_imag = to_image(grad)
    curvature = jnp.sum(ramp_weights * (image_real * image_real + image_imag * image_imag))
    grad_norm = jnp.sum(grad * grad)
    by_owner = misfit_table.reshape(ang_count, per_dev, sl_count, rows_dev)
    by_owner = jnp.swapaxes(by_owner, 1, 2).reshape(ang_count * sl_count, per_dev * rows_dev)
    scalars = jnp.broadcast_to(jnp.stack([grad_norm, curvature])[None], (ang_count * sl_count, 2))
    payload = jnp.concatenate([by_owner, scalars], axis=1)
    received = lax.all_to_all(payload, ANG_SL, 0, 0, tiled=True)
    totals = jnp.sum(received, axis=0)
    misfit = totals[: per_dev * rows_dev].reshape(per_dev, rows_dev)
    step_size = totals[per_dev * rows_dev] / (totals[per_dev * rows_dev + 1] + small_eps)
    updated = coefficients - step_size * grad.reshape(coefficients.shape)
    return (updated, misfit)


def solution(mesh):
    torus = Mesh(
        mesh.devices.reshape(8, 2, 4, 2, mesh.shape["sl"]),
        ("ang_0", "ang_1", "ang_2", "ang_3", "sl"),
    )
    in_specs = (P(ANG, "sl", None), P(), P(ANG), P(), P(None, None, ANG_SL, None))
    out_specs = (P(None, None, ANG_SL, None), P(ANG, "sl"))
    return jax.shard_map(
        shards, mesh=torus, in_specs=in_specs, out_specs=out_specs, check_vma=False
    )
```

```python
import math

import jax
import jax.numpy as jnp
from jax import lax
from jax.sharding import Mesh
from jax.sharding import PartitionSpec as P


W = 8192
HALF = 4096
K = 4096
EXTRA = 256
RAMP = 64
ROWS = 8
ANG = ("ang_0", "ang_1", "ang_2", "ang_3")
ANG_SL = ("ang_0", "ang_1", "ang_2", "ang_3", "sl")


paganin_strength = 16.0
small_eps = 1e-06
highest = lax.Precision.HIGHEST


def from_behind(value, axis, steps):
    count = lax.axis_size(axis)
    pairs = [(source, (source + steps) % count) for source in range(count)]
    return lax.ppermute(value, axis, pairs)


def paganin_rows(frequencies):
    row_ids = jnp.arange(ROWS, dtype=jnp.int32)
    row_offset = (row_ids[:, None] - row_ids[None, :]) % ROWS
    cos_table = jnp.cos(
        2.0
        * math.pi
        / ROWS
        * (row_ids[:, None, None] * row_offset[None, :, :] % ROWS).astype(jnp.float32)
    )
    row_freq = jnp.minimum(row_ids, ROWS - row_ids).astype(jnp.float32) / ROWS
    col_freq = frequencies / W
    damping = 1.0 / (
        1.0
        + paganin_strength
        * (col_freq[:, None] * col_freq[:, None] + row_freq[None, :] * row_freq[None, :])
    )
    return jnp.einsum("nq,qij->nij", damping, cos_table, precision=highest) / ROWS


def blend_band(projections, mirrored, offsets):
    position = jnp.arange(EXTRA, dtype=jnp.int32).astype(jnp.float32)
    weight = jnp.clip((position[None, :] - offsets[:, None].astype(jnp.float32)) / RAMP, 0.0, 1.0)
    own_band = projections[:, :, HALF - EXTRA : HALF]
    blended = own_band + weight[:, None, :] * (mirrored - own_band)
    return jnp.concatenate([projections[:, :, : HALF - EXTRA], blended], axis=2)


def spectrum_of(stitched):
    row_count = stitched.shape[0] * stitched.shape[1]
    low_split = W // 128
    outer_count = HALF // low_split
    high_count = K // 128
    folded = stitched.reshape(row_count, outer_count, low_split)
    norm_scale = 1.0 / math.sqrt(HALF)
    outer_ids = jnp.arange(outer_count, dtype=jnp.int32)
    lane_ids = jnp.arange(128, dtype=jnp.int32)
    first_phase = (
        2.0 * math.pi / 128 * (outer_ids[:, None] * lane_ids[None, :] % 128).astype(jnp.float32)
    )
    first_cos = jnp.cos(first_phase) * norm_scale
    first_sin = jnp.sin(first_phase) * norm_scale
    part_real = jnp.einsum("rab,ap->rbp", folded, first_cos, precision=highest)
    part_imag = -jnp.einsum("rab,ap->rbp", folded, first_sin, precision=highest)
    low_ids = jnp.arange(low_split, dtype=jnp.int32)
    twist_phase = 2.0 * math.pi / W * (low_ids[:, None] * lane_ids[None, :]).astype(jnp.float32)
    twist_cos = jnp.cos(twist_phase)
    twist_sin = jnp.sin(twist_phase)
    turned_real = part_real * twist_cos + part_imag * twist_sin
    turned_imag = part_imag * twist_cos - part_real * twist_sin
    high_ids = jnp.arange(high_count, dtype=jnp.int32)
    last_phase = (
        2.0
        * math.pi
        / low_split
        * (low_ids[:, None] * high_ids[None, :] % low_split).astype(jnp.float32)
    )
    last_cos = jnp.cos(last_phase)
    last_sin = jnp.sin(last_phase)
    spec_real = jnp.einsum("rbp,bq->rqp", turned_real, last_cos, precision=highest) + jnp.einsum(
        "rbp,bq->rqp", turned_imag, last_sin, precision=highest
    )
    spec_imag = jnp.einsum("rbp,bq->rqp", turned_imag, last_cos, precision=highest) - jnp.einsum(
        "rbp,bq->rqp", turned_real, last_sin, precision=highest
    )
    return (spec_real, spec_imag)


def step_body(projections, partner, offsets, angles, coefficients):
    ang_count = lax.axis_size(ANG)
    sl_count = lax.axis_size("sl")
    ang_index = lax.axis_index(ANG)
    sl_index = lax.axis_index("sl")
    per_dev = projections.shape[0]
    rows_dev = projections.shape[1]
    total_angles = per_dev * ang_count
    block_freqs = coefficients.shape[2]
    harmonics = coefficients.shape[3]
    columns = ROWS * block_freqs
    own_partners = lax.dynamic_slice_in_dim(partner, ang_index * per_dev, per_dev)
    across_dev = (ang_index + ang_count // 2) % ang_count
    partner_slots = own_partners - across_dev * per_dev
    arrived = from_behind(projections[:, :, HALF:], ANG, ang_count // 2)
    mirrored = jnp.flip(jnp.take(arrived, partner_slots, axis=0), axis=2)
    stitched = blend_band(projections, mirrored, offsets)
    spec_real, spec_imag = spectrum_of(stitched)
    spectra = jnp.stack([spec_real, spec_imag])
    dev_count = ang_count * sl_count
    lane_split = 128 // block_freqs
    spectra = spectra.reshape(2, per_dev * rows_dev, K // 128, lane_split, block_freqs)
    payload = spectra.transpose(2, 3, 0, 1, 4).reshape(dev_count, -1)
    received = lax.all_to_all(payload, ANG_SL, 0, 0, tiled=True)
    received = received.reshape(ang_count, sl_count, 2, per_dev, rows_dev * block_freqs)
    freq_major = received.transpose(2, 0, 3, 1, 4).reshape(2, total_angles, columns)
    freq_base = (ang_index * sl_count + sl_index) * block_freqs
    local_freq = (freq_base + jnp.arange(block_freqs, dtype=jnp.int32)).astype(jnp.float32)
    col_freq = jnp.tile(local_freq, ROWS)
    turn_phase = 2.0 * math.pi / W * col_freq
    turn_cos = jnp.cos(turn_phase)
    turn_sin = jnp.sin(turn_phase)
    own_real = freq_major[0]
    own_imag = freq_major[1]
    swap = (partner[:, None] == jnp.arange(total_angles, dtype=jnp.int32)[None, :]).astype(jnp.float32)
    own_both = jnp.concatenate([own_real, own_imag], axis=1)
    pair_both = jnp.dot(swap, own_both, precision=highest)
    pair_real = pair_both[:, :columns]
    pair_imag = pair_both[:, columns:]
    comb_real = own_real + turn_cos * pair_real + turn_sin * pair_imag
    comb_imag = own_imag + turn_sin * pair_real - turn_cos * pair_imag
    rows_matrix = paganin_rows(local_freq)
    full_matrix = jnp.einsum(
        "nij,mn->jmin", rows_matrix, jnp.eye(block_freqs, dtype=jnp.float32)
    ).reshape(columns, columns)
    filt_real = jnp.dot(comb_real, full_matrix, precision=highest)
    filt_imag = jnp.dot(comb_imag, full_matrix, precision=highest)
    ramp_weights = (col_freq + 0.5) / K
    coef_rows = coefficients.reshape(2 * columns, harmonics)
    harm_shift = (jnp.arange(harmonics, dtype=jnp.int32) - harmonics // 2).astype(jnp.float32)
    norm_scale = 1.0 / math.sqrt(harmonics)
    phase_tab = angles[:, None] * harm_shift[None, :]
    tabs = jnp.concatenate(
        [jnp.cos(phase_tab) * norm_scale, jnp.sin(phase_tab) * norm_scale]
    )

    def to_image(coef):
        prod = lax.dot_general(
            tabs, coef, (((1,), (1,)), ((), ())), precision=highest
        )
        cos_part, sin_part = prod[:total_angles], prod[total_angles:]
        real = cos_part[:, :columns] - sin_part[:, columns:]
        imag = cos_part[:, columns:] + sin_part[:, :columns]
        return real, imag

    model_real, model_imag = to_image(coef_rows)
    diff_real = model_real - filt_real
    diff_imag = model_imag - filt_imag
    resid_real = ramp_weights * diff_real
    resid_imag = ramp_weights * diff_imag
    energy = (diff_real * resid_real + diff_imag * resid_imag).reshape(
        total_angles, ROWS, block_freqs
    )
    misfit_table = jnp.sum(energy, axis=2) / K
    stacked = jnp.concatenate(
        [
            jnp.concatenate([resid_real, resid_imag], axis=1),
            jnp.concatenate([resid_imag, -resid_real], axis=1),
        ]
    )
    gram = lax.dot_general(tabs, tabs, (((1,), (1,)), ((), ())), precision=highest)
    gram_real = gram[:total_angles, :total_angles] + gram[total_angles:, total_angles:]
    gram_imag = gram[total_angles:, :total_angles] - gram[:total_angles, total_angles:]
    gram_both = jnp.concatenate(
        [
            jnp.concatenate([gram_real, -gram_imag], axis=1),
            jnp.concatenate([gram_imag, gram_real], axis=1),
        ]
    )
    resid_both = jnp.concatenate([resid_real, resid_imag])
    image_both = jnp.dot(gram_both, resid_both, precision=highest)
    image_real, image_imag = image_both[:total_angles], image_both[total_angles:]
    curvature = jnp.sum(ramp_weights * (image_real * image_real + image_imag * image_imag))
    grad_norm = jnp.sum(resid_real * image_real + resid_imag * image_imag)
    by_owner = misfit_table.reshape(ang_count, per_dev, sl_count, rows_dev)
    by_owner = jnp.swapaxes(by_owner, 1, 2).reshape(ang_count * sl_count, per_dev * rows_dev)
    scalars = jnp.broadcast_to(jnp.stack([grad_norm, curvature])[None], (ang_count * sl_count, 2))
    payload = jnp.concatenate([by_owner, scalars], axis=1)
    received = lax.all_to_all(payload, ANG_SL, 0, 0, tiled=True)
    totals = jnp.sum(received, axis=0)
    misfit = totals[: per_dev * rows_dev].reshape(per_dev, rows_dev)
    step_size = totals[per_dev * rows_dev] / (totals[per_dev * rows_dev + 1] + small_eps)
    grad = lax.dot_general(stacked, tabs, (((0,), (0,)), ((), ())), precision=highest)
    updated = coefficients - step_size * grad.reshape(coefficients.shape)
    return (updated, misfit)


def solution(mesh):
    torus = Mesh(
        mesh.devices.reshape(8, 2, 4, 2, mesh.shape["sl"]),
        ("ang_0", "ang_1", "ang_2", "ang_3", "sl"),
    )
    in_specs = (P(ANG, "sl", None), P(), P(ANG), P(), P(None, None, ANG_SL, None))
    out_specs = (P(None, None, ANG_SL, None), P(ANG, "sl"))
    return jax.shard_map(
        step_body, mesh=torus, in_specs=in_specs, out_specs=out_specs, check_vma=False
    )
```

```python
import math

import jax
import jax.numpy as jnp
from jax import lax
from jax.sharding import Mesh
from jax.sharding import PartitionSpec as P


W = 8192
HALF = 4096
K = 4096
EXTRA = 256
RAMP = 64
ROWS = 8
ANG = ("ang_0", "ang_1", "ang_2", "ang_3")
ANG_SL = ("ang_0", "ang_1", "ang_2", "ang_3", "sl")


paganin_strength = 16.0
small_eps = 1e-06
highest = lax.Precision.HIGHEST


def from_behind(value, axis, steps):
    count = lax.axis_size(axis)
    pairs = [(source, (source + steps) % count) for source in range(count)]
    return lax.ppermute(value, axis, pairs)


def paganin_rows(frequencies):
    row_ids = jnp.arange(ROWS, dtype=jnp.int32)
    row_offset = (row_ids[:, None] - row_ids[None, :]) % ROWS
    cos_table = jnp.cos(
        2.0
        * math.pi
        / ROWS
        * (row_ids[:, None, None] * row_offset[None, :, :] % ROWS).astype(jnp.float32)
    )
    row_freq = jnp.minimum(row_ids, ROWS - row_ids).astype(jnp.float32) / ROWS
    col_freq = frequencies / W
    damping = 1.0 / (
        1.0
        + paganin_strength
        * (col_freq[:, None] * col_freq[:, None] + row_freq[None, :] * row_freq[None, :])
    )
    return jnp.einsum("nq,qij->nij", damping, cos_table, precision=highest) / ROWS


def blend_band(projections, mirrored, offsets):
    position = jnp.arange(EXTRA, dtype=jnp.int32).astype(jnp.float32)
    weight = jnp.clip((position[None, :] - offsets[:, None].astype(jnp.float32)) / RAMP, 0.0, 1.0)
    own_band = projections[:, :, HALF - EXTRA : HALF]
    blended = own_band + weight[:, None, :] * (mirrored - own_band)
    return jnp.concatenate([projections[:, :, : HALF - EXTRA], blended], axis=2)


def spectrum_of(stitched):
    row_count = stitched.shape[0] * stitched.shape[1]
    low_split = W // 128
    outer_count = HALF // low_split
    high_count = K // 128
    folded = stitched.reshape(row_count, outer_count, low_split)
    norm_scale = 1.0 / math.sqrt(HALF)
    outer_ids = jnp.arange(outer_count, dtype=jnp.int32)
    lane_ids = jnp.arange(128, dtype=jnp.int32)
    first_phase = (
        2.0 * math.pi / 128 * (outer_ids[:, None] * lane_ids[None, :] % 128).astype(jnp.float32)
    )
    first_cos = jnp.cos(first_phase) * norm_scale
    first_sin = jnp.sin(first_phase) * norm_scale
    part_real = jnp.einsum("rab,ap->rbp", folded, first_cos, precision=highest)
    part_imag = -jnp.einsum("rab,ap->rbp", folded, first_sin, precision=highest)
    low_ids = jnp.arange(low_split, dtype=jnp.int32)
    twist_phase = 2.0 * math.pi / W * (low_ids[:, None] * lane_ids[None, :]).astype(jnp.float32)
    twist_cos = jnp.cos(twist_phase)
    twist_sin = jnp.sin(twist_phase)
    turned_real = part_real * twist_cos + part_imag * twist_sin
    turned_imag = part_imag * twist_cos - part_real * twist_sin
    high_ids = jnp.arange(high_count, dtype=jnp.int32)
    last_phase = (
        2.0
        * math.pi
        / low_split
        * (low_ids[:, None] * high_ids[None, :] % low_split).astype(jnp.float32)
    )
    last_cos = jnp.cos(last_phase)
    last_sin = jnp.sin(last_phase)
    spec_real = jnp.einsum("rbp,bq->rqp", turned_real, last_cos, precision=highest) + jnp.einsum(
        "rbp,bq->rqp", turned_imag, last_sin, precision=highest
    )
    spec_imag = jnp.einsum("rbp,bq->rqp", turned_imag, last_cos, precision=highest) - jnp.einsum(
        "rbp,bq->rqp", turned_real, last_sin, precision=highest
    )
    return (spec_real, spec_imag)


def step_body(projections, partner, offsets, angles, coefficients):
    ang_count = lax.axis_size(ANG)
    sl_count = lax.axis_size("sl")
    ang_index = lax.axis_index(ANG)
    sl_index = lax.axis_index("sl")
    per_dev = projections.shape[0]
    rows_dev = projections.shape[1]
    total_angles = per_dev * ang_count
    block_freqs = coefficients.shape[2]
    harmonics = coefficients.shape[3]
    columns = ROWS * block_freqs
    own_partners = lax.dynamic_slice_in_dim(partner, ang_index * per_dev, per_dev)
    across_dev = (ang_index + ang_count // 2) % ang_count
    partner_slots = own_partners - across_dev * per_dev
    arrived = from_behind(projections[:, :, HALF:], ANG, ang_count // 2)
    mirrored = jnp.flip(jnp.take(arrived, partner_slots, axis=0), axis=2)
    stitched = blend_band(projections, mirrored, offsets)
    spec_real, spec_imag = spectrum_of(stitched)
    spectra = jnp.stack([spec_real, spec_imag])
    dev_count = ang_count * sl_count
    lane_split = 128 // block_freqs
    spectra = spectra.reshape(2, per_dev * rows_dev, K // 128, lane_split, block_freqs)
    payload = spectra.transpose(2, 3, 0, 1, 4).reshape(dev_count, -1)
    received = lax.all_to_all(payload, ANG_SL, 0, 0, tiled=True)
    if per_dev == 2 and sl_count == 2:
        half = rows_dev * block_freqs
        row_ids = jnp.arange(dev_count, dtype=jnp.int32)
        lane_ids = jnp.arange(2 * columns, dtype=jnp.int32)
        row_swap = ((row_ids[:, None] ^ 1) == row_ids[None, :]).astype(jnp.float32)
        lane_swap = ((lane_ids[:, None] ^ half) == lane_ids[None, :]).astype(jnp.float32)
        swapped = jnp.dot(
            row_swap, jnp.dot(received, lane_swap, precision=highest), precision=highest
        )
        same_half = (row_ids[:, None] % 2) == ((lane_ids[None, :] // half) % 2)
        own_both = jnp.where(same_half, received, swapped)
    else:
        received = received.reshape(ang_count, sl_count, 2, per_dev, rows_dev * block_freqs)
        own_both = received.transpose(0, 3, 2, 1, 4).reshape(total_angles, 2 * columns)
    freq_base = (ang_index * sl_count + sl_index) * block_freqs
    local_freq = (freq_base + jnp.arange(block_freqs, dtype=jnp.int32)).astype(jnp.float32)
    col_freq = jnp.tile(local_freq, ROWS)
    turn_phase = 2.0 * math.pi / W * col_freq
    turn_cos = jnp.cos(turn_phase)
    turn_sin = jnp.sin(turn_phase)
    own_real = own_both[:, :columns]
    own_imag = own_both[:, columns:]
    swap = (partner[:, None] == jnp.arange(total_angles, dtype=jnp.int32)[None, :]).astype(jnp.float32)
    pair_both = jnp.dot(swap, own_both, precision=highest)
    pair_real = pair_both[:, :columns]
    pair_imag = pair_both[:, columns:]
    comb_real = own_real + turn_cos * pair_real + turn_sin * pair_imag
    comb_imag = own_imag + turn_sin * pair_real - turn_cos * pair_imag
    rows_matrix = paganin_rows(local_freq)
    full_matrix = jnp.einsum(
        "nij,mn->jmin", rows_matrix, jnp.eye(block_freqs, dtype=jnp.float32)
    ).reshape(columns, columns)
    filt_real = jnp.dot(comb_real, full_matrix, precision=highest)
    filt_imag = jnp.dot(comb_imag, full_matrix, precision=highest)
    ramp_weights = (col_freq + 0.5) / K
    coef_rows = coefficients.reshape(2 * columns, harmonics)
    harm_shift = (jnp.arange(harmonics, dtype=jnp.int32) - harmonics // 2).astype(jnp.float32)
    norm_scale = 1.0 / math.sqrt(harmonics)
    phase_tab = angles[:, None] * harm_shift[None, :]
    tabs = jnp.concatenate(
        [jnp.cos(phase_tab) * norm_scale, jnp.sin(phase_tab) * norm_scale]
    )

    def to_image(coef):
        prod = lax.dot_general(
            tabs, coef, (((1,), (1,)), ((), ())), precision=highest
        )
        cos_part, sin_part = prod[:total_angles], prod[total_angles:]
        real = cos_part[:, :columns] - sin_part[:, columns:]
        imag = cos_part[:, columns:] + sin_part[:, :columns]
        return real, imag

    model_real, model_imag = to_image(coef_rows)
    diff_real = model_real - filt_real
    diff_imag = model_imag - filt_imag
    resid_real = ramp_weights * diff_real
    resid_imag = ramp_weights * diff_imag
    energy = (diff_real * resid_real + diff_imag * resid_imag).reshape(
        total_angles, ROWS, block_freqs
    )
    misfit_table = jnp.sum(energy, axis=2) / K
    stacked = jnp.concatenate(
        [
            jnp.concatenate([resid_real, resid_imag], axis=1),
            jnp.concatenate([resid_imag, -resid_real], axis=1),
        ]
    )
    gram = lax.dot_general(tabs, tabs, (((1,), (1,)), ((), ())), precision=highest)
    gram_real = gram[:total_angles, :total_angles] + gram[total_angles:, total_angles:]
    gram_imag = gram[total_angles:, :total_angles] - gram[:total_angles, total_angles:]
    gram_both = jnp.concatenate(
        [
            jnp.concatenate([gram_real, -gram_imag], axis=1),
            jnp.concatenate([gram_imag, gram_real], axis=1),
        ]
    )
    resid_both = jnp.concatenate([resid_real, resid_imag])
    image_both = jnp.dot(gram_both, resid_both, precision=highest)
    image_real, image_imag = image_both[:total_angles], image_both[total_angles:]
    curvature = jnp.sum(ramp_weights * (image_real * image_real + image_imag * image_imag))
    grad_norm = jnp.sum(resid_real * image_real + resid_imag * image_imag)
    by_owner = misfit_table.reshape(ang_count, per_dev, sl_count, rows_dev)
    by_owner = jnp.swapaxes(by_owner, 1, 2).reshape(ang_count * sl_count, per_dev * rows_dev)
    scalars = jnp.broadcast_to(jnp.stack([grad_norm, curvature])[None], (ang_count * sl_count, 2))
    payload = jnp.concatenate([by_owner, scalars], axis=1)
    received = lax.all_to_all(payload, ANG_SL, 0, 0, tiled=True)
    totals = jnp.sum(received, axis=0)
    misfit = totals[: per_dev * rows_dev].reshape(per_dev, rows_dev)
    step_size = totals[per_dev * rows_dev] / (totals[per_dev * rows_dev + 1] + small_eps)
    grad = lax.dot_general(stacked, tabs, (((0,), (0,)), ((), ())), precision=highest)
    updated = coefficients - step_size * grad.reshape(coefficients.shape)
    return (updated, misfit)


def solution(mesh):
    torus = Mesh(
        mesh.devices.reshape(8, 2, 4, 2, mesh.shape["sl"]),
        ("ang_0", "ang_1", "ang_2", "ang_3", "sl"),
    )
    in_specs = (P(ANG, "sl", None), P(), P(ANG), P(), P(None, None, ANG_SL, None))
    out_specs = (P(None, None, ANG_SL, None), P(ANG, "sl"))
    return jax.shard_map(
        step_body, mesh=torus, in_specs=in_specs, out_specs=out_specs, check_vma=False
    )
```

```python
import math

import jax
import jax.numpy as jnp
from jax import lax
from jax.sharding import Mesh
from jax.sharding import PartitionSpec as P


W = 8192
HALF = 4096
K = 4096
EXTRA = 256
RAMP = 64
ROWS = 8
ANG = ("ang_0", "ang_1", "ang_2", "ang_3")
ANG_SL = ("ang_0", "ang_1", "ang_2", "ang_3", "sl")


paganin_strength = 16.0
small_eps = 1e-06
highest = lax.Precision.HIGHEST


def from_behind(value, axis, steps):
    count = lax.axis_size(axis)
    pairs = [(source, (source + steps) % count) for source in range(count)]
    return lax.ppermute(value, axis, pairs)


def paganin_rows(frequencies):
    row_ids = jnp.arange(ROWS, dtype=jnp.int32)
    row_offset = (row_ids[:, None] - row_ids[None, :]) % ROWS
    cos_table = jnp.cos(
        2.0
        * math.pi
        / ROWS
        * (row_ids[:, None, None] * row_offset[None, :, :] % ROWS).astype(jnp.float32)
    )
    row_freq = jnp.minimum(row_ids, ROWS - row_ids).astype(jnp.float32) / ROWS
    col_freq = frequencies / W
    damping = 1.0 / (
        1.0
        + paganin_strength
        * (col_freq[:, None] * col_freq[:, None] + row_freq[None, :] * row_freq[None, :])
    )
    return jnp.einsum("nq,qij->nij", damping, cos_table, precision=highest) / ROWS


def blend_band(projections, mirrored, offsets):
    position = jnp.arange(EXTRA, dtype=jnp.int32).astype(jnp.float32)
    weight = jnp.clip((position[None, :] - offsets[:, None].astype(jnp.float32)) / RAMP, 0.0, 1.0)
    own_band = projections[:, :, HALF - EXTRA : HALF]
    blended = own_band + weight[:, None, :] * (mirrored - own_band)
    return jnp.concatenate([projections[:, :, : HALF - EXTRA], blended], axis=2)


def spectrum_of(stitched):
    row_count = stitched.shape[0] * stitched.shape[1]
    low_split = W // 128
    outer_count = HALF // low_split
    high_count = K // 128
    folded = stitched.reshape(row_count, outer_count, low_split)
    norm_scale = 1.0 / math.sqrt(HALF)
    outer_ids = jnp.arange(outer_count, dtype=jnp.int32)
    lane_ids = jnp.arange(128, dtype=jnp.int32)
    first_phase = (
        2.0 * math.pi / 128 * (outer_ids[:, None] * lane_ids[None, :] % 128).astype(jnp.float32)
    )
    first_cos = jnp.cos(first_phase) * norm_scale
    first_sin = jnp.sin(first_phase) * norm_scale
    part_real = jnp.einsum("rab,ap->rbp", folded, first_cos, precision=highest)
    part_imag = -jnp.einsum("rab,ap->rbp", folded, first_sin, precision=highest)
    low_ids = jnp.arange(low_split, dtype=jnp.int32)
    twist_phase = 2.0 * math.pi / W * (low_ids[:, None] * lane_ids[None, :]).astype(jnp.float32)
    twist_cos = jnp.cos(twist_phase)
    twist_sin = jnp.sin(twist_phase)
    turned_real = part_real * twist_cos + part_imag * twist_sin
    turned_imag = part_imag * twist_cos - part_real * twist_sin
    high_ids = jnp.arange(high_count, dtype=jnp.int32)
    last_phase = (
        2.0
        * math.pi
        / low_split
        * (low_ids[:, None] * high_ids[None, :] % low_split).astype(jnp.float32)
    )
    last_cos = jnp.cos(last_phase)
    last_sin = jnp.sin(last_phase)
    spec_real = jnp.einsum("rbp,bq->rqp", turned_real, last_cos, precision=highest) + jnp.einsum(
        "rbp,bq->rqp", turned_imag, last_sin, precision=highest
    )
    spec_imag = jnp.einsum("rbp,bq->rqp", turned_imag, last_cos, precision=highest) - jnp.einsum(
        "rbp,bq->rqp", turned_real, last_sin, precision=highest
    )
    return (spec_real, spec_imag)


def step_body(projections, partner, offsets, angles, coefficients):
    ang_count = lax.axis_size(ANG)
    sl_count = lax.axis_size("sl")
    ang_index = lax.axis_index(ANG)
    sl_index = lax.axis_index("sl")
    per_dev = projections.shape[0]
    rows_dev = projections.shape[1]
    total_angles = per_dev * ang_count
    block_freqs = coefficients.shape[2]
    harmonics = coefficients.shape[3]
    columns = ROWS * block_freqs
    own_partners = lax.dynamic_slice_in_dim(partner, ang_index * per_dev, per_dev)
    across_dev = (ang_index + ang_count // 2) % ang_count
    partner_slots = own_partners - across_dev * per_dev
    arrived = from_behind(projections[:, :, HALF:], ANG, ang_count // 2)
    mirrored = jnp.flip(jnp.take(arrived, partner_slots, axis=0), axis=2)
    stitched = blend_band(projections, mirrored, offsets)
    spec_real, spec_imag = spectrum_of(stitched)
    spectra = jnp.stack([spec_real, spec_imag])
    dev_count = ang_count * sl_count
    lane_split = 128 // block_freqs
    spectra = spectra.reshape(2, per_dev * rows_dev, K // 128, lane_split, block_freqs)
    payload = spectra.transpose(2, 3, 0, 1, 4).reshape(dev_count, -1)
    received = lax.all_to_all(payload, ANG_SL, 0, 0, tiled=True)
    if per_dev == 2 and sl_count == 2:
        half = rows_dev * block_freqs
        row_ids = jnp.arange(dev_count, dtype=jnp.int32)
        lane_ids = jnp.arange(2 * columns, dtype=jnp.int32)
        row_swap = ((row_ids[:, None] ^ 1) == row_ids[None, :]).astype(jnp.float32)
        lane_swap = ((lane_ids[:, None] ^ half) == lane_ids[None, :]).astype(jnp.float32)
        swapped = jnp.dot(
            row_swap, jnp.dot(received, lane_swap, precision=highest), precision=highest
        )
        same_half = (row_ids[:, None] % 2) == ((lane_ids[None, :] // half) % 2)
        own_both = jnp.where(same_half, received, swapped)
    else:
        received = received.reshape(ang_count, sl_count, 2, per_dev, rows_dev * block_freqs)
        own_both = received.transpose(0, 3, 2, 1, 4).reshape(total_angles, 2 * columns)
    freq_base = (ang_index * sl_count + sl_index) * block_freqs
    local_freq = (freq_base + jnp.arange(block_freqs, dtype=jnp.int32)).astype(jnp.float32)
    col_freq = jnp.tile(local_freq, ROWS)
    turn_phase = 2.0 * math.pi / W * col_freq
    turn_cos = jnp.cos(turn_phase)
    turn_sin = jnp.sin(turn_phase)
    own_real = own_both[:, :columns]
    own_imag = own_both[:, columns:]
    swap = (partner[:, None] == jnp.arange(total_angles, dtype=jnp.int32)[None, :]).astype(jnp.float32)
    pair_both = jnp.dot(swap, own_both, precision=highest)
    pair_real = pair_both[:, :columns]
    pair_imag = pair_both[:, columns:]
    comb_real = own_real + turn_cos * pair_real + turn_sin * pair_imag
    comb_imag = own_imag + turn_sin * pair_real - turn_cos * pair_imag
    rows_matrix = paganin_rows(local_freq)
    full_matrix = jnp.einsum(
        "nij,mn->jmin", rows_matrix, jnp.eye(block_freqs, dtype=jnp.float32)
    ).reshape(columns, columns)
    filt_real = jnp.dot(comb_real, full_matrix, precision=highest)
    filt_imag = jnp.dot(comb_imag, full_matrix, precision=highest)
    ramp_weights = (col_freq + 0.5) / K
    coef_rows = coefficients.reshape(2 * columns, harmonics)
    harm_shift = (jnp.arange(harmonics, dtype=jnp.int32) - harmonics // 2).astype(jnp.float32)
    norm_scale = 1.0 / math.sqrt(harmonics)
    phase_tab = angles[:, None] * harm_shift[None, :]
    tabs = jnp.concatenate(
        [jnp.cos(phase_tab) * norm_scale, jnp.sin(phase_tab) * norm_scale]
    )

    def to_image(coef):
        prod = lax.dot_general(
            tabs, coef, (((1,), (1,)), ((), ())), precision=highest
        )
        cos_part, sin_part = prod[:total_angles], prod[total_angles:]
        real = cos_part[:, :columns] - sin_part[:, columns:]
        imag = cos_part[:, columns:] + sin_part[:, :columns]
        return real, imag

    model_real, model_imag = to_image(coef_rows)
    diff_real = model_real - filt_real
    diff_imag = model_imag - filt_imag
    resid_real = ramp_weights * diff_real
    resid_imag = ramp_weights * diff_imag
    energy = (diff_real * resid_real + diff_imag * resid_imag).reshape(
        total_angles, ROWS, block_freqs
    )
    misfit_table = jnp.sum(energy, axis=2) / K
    stacked = jnp.concatenate(
        [
            jnp.concatenate([resid_real, resid_imag], axis=1),
            jnp.concatenate([resid_imag, -resid_real], axis=1),
        ]
    )
    gram = lax.dot_general(tabs, tabs, (((1,), (1,)), ((), ())), precision=highest)
    gram_real = gram[:total_angles, :total_angles] + gram[total_angles:, total_angles:]
    gram_imag = gram[total_angles:, :total_angles] - gram[:total_angles, total_angles:]
    gram_both = jnp.concatenate(
        [
            jnp.concatenate([gram_real, -gram_imag], axis=1),
            jnp.concatenate([gram_imag, gram_real], axis=1),
        ]
    )
    resid_both = jnp.concatenate([resid_real, resid_imag])
    image_both = jnp.dot(gram_both, resid_both, precision=lax.Precision.HIGH)
    image_real, image_imag = image_both[:total_angles], image_both[total_angles:]
    curvature = jnp.sum(ramp_weights * (image_real * image_real + image_imag * image_imag))
    grad_norm = jnp.sum(resid_real * image_real + resid_imag * image_imag)
    by_owner = misfit_table.reshape(ang_count, per_dev, sl_count, rows_dev)
    by_owner = jnp.swapaxes(by_owner, 1, 2).reshape(ang_count * sl_count, per_dev * rows_dev)
    scalars = jnp.broadcast_to(jnp.stack([grad_norm, curvature])[None], (ang_count * sl_count, 2))
    payload = jnp.concatenate([by_owner, scalars], axis=1)
    received = lax.all_to_all(payload, ANG_SL, 0, 0, tiled=True)
    totals = jnp.sum(received, axis=0)
    misfit = totals[: per_dev * rows_dev].reshape(per_dev, rows_dev)
    step_size = totals[per_dev * rows_dev] / (totals[per_dev * rows_dev + 1] + small_eps)
    step_grad = lax.dot_general(
        -step_size * stacked, tabs, (((0,), (0,)), ((), ())), precision=lax.Precision.HIGH
    )
    updated = coefficients + step_grad.reshape(coefficients.shape)
    return (updated, misfit)


def solution(mesh):
    torus = Mesh(
        mesh.devices.reshape(8, 2, 4, 2, mesh.shape["sl"]),
        ("ang_0", "ang_1", "ang_2", "ang_3", "sl"),
    )
    in_specs = (P(ANG, "sl", None), P(), P(ANG), P(), P(None, None, ANG_SL, None))
    out_specs = (P(None, None, ANG_SL, None), P(ANG, "sl"))
    return jax.shard_map(
        step_body, mesh=torus, in_specs=in_specs, out_specs=out_specs, check_vma=False
    )
```

```python
import math

import jax
import jax.numpy as jnp
from jax import lax
from jax.sharding import Mesh
from jax.sharding import PartitionSpec as P


W = 8192
HALF = 4096
K = 4096
EXTRA = 256
RAMP = 64
ROWS = 8
ANG = ("ang_0", "ang_1", "ang_2", "ang_3")
ANG_SL = ("ang_0", "ang_1", "ang_2", "ang_3", "sl")


paganin_strength = 16.0
small_eps = 1e-06
highest = lax.Precision.HIGHEST


def from_behind(value, axis, steps):
    count = lax.axis_size(axis)
    pairs = [(source, (source + steps) % count) for source in range(count)]
    return lax.ppermute(value, axis, pairs)


def paganin_rows(frequencies):
    row_ids = jnp.arange(ROWS, dtype=jnp.int32)
    row_offset = (row_ids[:, None] - row_ids[None, :]) % ROWS
    cos_table = jnp.cos(
        2.0
        * math.pi
        / ROWS
        * (row_ids[:, None, None] * row_offset[None, :, :] % ROWS).astype(jnp.float32)
    )
    row_freq = jnp.minimum(row_ids, ROWS - row_ids).astype(jnp.float32) / ROWS
    col_freq = frequencies / W
    damping = 1.0 / (
        1.0
        + paganin_strength
        * (col_freq[:, None] * col_freq[:, None] + row_freq[None, :] * row_freq[None, :])
    )
    return jnp.einsum("nq,qij->nij", damping, cos_table, precision=highest) / ROWS


def blend_band(projections, mirrored, offsets):
    position = jnp.arange(EXTRA, dtype=jnp.int32).astype(jnp.float32)
    weight = jnp.clip((position[None, :] - offsets[:, None].astype(jnp.float32)) / RAMP, 0.0, 1.0)
    own_band = projections[:, :, HALF - EXTRA : HALF]
    blended = own_band + weight[:, None, :] * (mirrored - own_band)
    return jnp.concatenate([projections[:, :, : HALF - EXTRA], blended], axis=2)


def spectrum_of(stitched):
    row_count = stitched.shape[0] * stitched.shape[1]
    low_split = W // 128
    outer_count = HALF // low_split
    high_count = K // 128
    folded = stitched.reshape(row_count, outer_count, low_split)
    norm_scale = 1.0 / math.sqrt(HALF)
    outer_ids = jnp.arange(outer_count, dtype=jnp.int32)
    lane_ids = jnp.arange(128, dtype=jnp.int32)
    first_phase = (
        2.0 * math.pi / 128 * (outer_ids[:, None] * lane_ids[None, :] % 128).astype(jnp.float32)
    )
    first_cos = jnp.cos(first_phase) * norm_scale
    first_sin = jnp.sin(first_phase) * norm_scale
    part_real = jnp.einsum("rab,ap->rbp", folded, first_cos, precision=highest)
    part_imag = -jnp.einsum("rab,ap->rbp", folded, first_sin, precision=highest)
    low_ids = jnp.arange(low_split, dtype=jnp.int32)
    twist_phase = 2.0 * math.pi / W * (low_ids[:, None] * lane_ids[None, :]).astype(jnp.float32)
    twist_cos = jnp.cos(twist_phase)
    twist_sin = jnp.sin(twist_phase)
    turned_real = part_real * twist_cos + part_imag * twist_sin
    turned_imag = part_imag * twist_cos - part_real * twist_sin
    high_ids = jnp.arange(high_count, dtype=jnp.int32)
    last_phase = (
        2.0
        * math.pi
        / low_split
        * (low_ids[:, None] * high_ids[None, :] % low_split).astype(jnp.float32)
    )
    last_cos = jnp.cos(last_phase)
    last_sin = jnp.sin(last_phase)
    spec_real = jnp.einsum("rbp,bq->rqp", turned_real, last_cos, precision=highest) + jnp.einsum(
        "rbp,bq->rqp", turned_imag, last_sin, precision=highest
    )
    spec_imag = jnp.einsum("rbp,bq->rqp", turned_imag, last_cos, precision=highest) - jnp.einsum(
        "rbp,bq->rqp", turned_real, last_sin, precision=highest
    )
    return (spec_real, spec_imag)


def step_body(projections, partner, offsets, angles, coefficients):
    ang_count = lax.axis_size(ANG)
    sl_count = lax.axis_size("sl")
    ang_index = lax.axis_index(ANG)
    sl_index = lax.axis_index("sl")
    per_dev = projections.shape[0]
    rows_dev = projections.shape[1]
    total_angles = per_dev * ang_count
    block_freqs = coefficients.shape[2]
    harmonics = coefficients.shape[3]
    columns = ROWS * block_freqs
    own_partners = lax.dynamic_slice_in_dim(partner, ang_index * per_dev, per_dev)
    across_dev = (ang_index + ang_count // 2) % ang_count
    partner_slots = own_partners - across_dev * per_dev
    arrived = from_behind(projections[:, :, HALF:], ANG, ang_count // 2)
    chosen = arrived[0]
    for slot in range(1, per_dev):
        chosen = jnp.where((partner_slots == slot)[:, None, None], arrived[slot], chosen)
    mirrored = jnp.flip(chosen, axis=2)
    stitched = blend_band(projections, mirrored, offsets)
    spec_real, spec_imag = spectrum_of(stitched)
    spectra = jnp.stack([spec_real, spec_imag])
    dev_count = ang_count * sl_count
    lane_split = 128 // block_freqs
    spectra = spectra.reshape(2, per_dev * rows_dev, K // 128, lane_split, block_freqs)
    payload = spectra.transpose(2, 3, 0, 1, 4).reshape(dev_count, -1)
    received = lax.all_to_all(payload, ANG_SL, 0, 0, tiled=True)
    if per_dev == 2 and sl_count == 2:
        half = rows_dev * block_freqs
        row_ids = jnp.arange(dev_count, dtype=jnp.int32)
        lane_ids = jnp.arange(2 * columns, dtype=jnp.int32)
        row_swap = ((row_ids[:, None] ^ 1) == row_ids[None, :]).astype(jnp.float32)
        lane_swap = ((lane_ids[:, None] ^ half) == lane_ids[None, :]).astype(jnp.float32)
        swapped = jnp.dot(
            row_swap, jnp.dot(received, lane_swap, precision=highest), precision=highest
        )
        same_half = (row_ids[:, None] % 2) == ((lane_ids[None, :] // half) % 2)
        own_both = jnp.where(same_half, received, swapped)
    else:
        received = received.reshape(ang_count, sl_count, 2, per_dev, rows_dev * block_freqs)
        own_both = received.transpose(0, 3, 2, 1, 4).reshape(total_angles, 2 * columns)
    freq_base = (ang_index * sl_count + sl_index) * block_freqs
    local_freq = (freq_base + jnp.arange(block_freqs, dtype=jnp.int32)).astype(jnp.float32)
    col_freq = jnp.tile(local_freq, ROWS)
    turn_phase = 2.0 * math.pi / W * col_freq
    turn_cos = jnp.cos(turn_phase)
    turn_sin = jnp.sin(turn_phase)
    own_real = own_both[:, :columns]
    own_imag = own_both[:, columns:]
    swap = (partner[:, None] == jnp.arange(total_angles, dtype=jnp.int32)[None, :]).astype(jnp.float32)
    pair_both = jnp.dot(swap, own_both, precision=highest)
    pair_real = pair_both[:, :columns]
    pair_imag = pair_both[:, columns:]
    comb_real = own_real + turn_cos * pair_real + turn_sin * pair_imag
    comb_imag = own_imag + turn_sin * pair_real - turn_cos * pair_imag
    rows_matrix = paganin_rows(local_freq)
    full_matrix = jnp.einsum(
        "nij,mn->jmin", rows_matrix, jnp.eye(block_freqs, dtype=jnp.float32)
    ).reshape(columns, columns)
    filt_real = jnp.dot(comb_real, full_matrix, precision=highest)
    filt_imag = jnp.dot(comb_imag, full_matrix, precision=highest)
    ramp_weights = (col_freq + 0.5) / K
    coef_rows = coefficients.reshape(2 * columns, harmonics)
    harm_shift = (jnp.arange(harmonics, dtype=jnp.int32) - harmonics // 2).astype(jnp.float32)
    norm_scale = 1.0 / math.sqrt(harmonics)
    phase_tab = angles[:, None] * harm_shift[None, :]
    tabs = jnp.concatenate(
        [jnp.cos(phase_tab) * norm_scale, jnp.sin(phase_tab) * norm_scale]
    )

    def to_image(coef):
        prod = lax.dot_general(
            tabs, coef, (((1,), (1,)), ((), ())), precision=highest
        )
        cos_part, sin_part = prod[:total_angles], prod[total_angles:]
        real = cos_part[:, :columns] - sin_part[:, columns:]
        imag = cos_part[:, columns:] + sin_part[:, :columns]
        return real, imag

    model_real, model_imag = to_image(coef_rows)
    diff_real = model_real - filt_real
    diff_imag = model_imag - filt_imag
    resid_real = ramp_weights * diff_real
    resid_imag = ramp_weights * diff_imag
    energy = (diff_real * resid_real + diff_imag * resid_imag).reshape(
        total_angles, ROWS, block_freqs
    )
    misfit_table = jnp.sum(energy, axis=2) / K
    stacked = jnp.concatenate(
        [
            jnp.concatenate([resid_real, resid_imag], axis=1),
            jnp.concatenate([resid_imag, -resid_real], axis=1),
        ]
    )
    gram = lax.dot_general(tabs, tabs, (((1,), (1,)), ((), ())), precision=highest)
    gram_real = gram[:total_angles, :total_angles] + gram[total_angles:, total_angles:]
    gram_imag = gram[total_angles:, :total_angles] - gram[:total_angles, total_angles:]
    gram_both = jnp.concatenate(
        [
            jnp.concatenate([gram_real, -gram_imag], axis=1),
            jnp.concatenate([gram_imag, gram_real], axis=1),
        ]
    )
    resid_both = jnp.concatenate([resid_real, resid_imag])
    image_both = jnp.dot(gram_both, resid_both, precision=lax.Precision.HIGH)
    image_real, image_imag = image_both[:total_angles], image_both[total_angles:]
    curvature = jnp.sum(ramp_weights * (image_real * image_real + image_imag * image_imag))
    grad_norm = jnp.sum(resid_real * image_real + resid_imag * image_imag)
    by_owner = misfit_table.reshape(ang_count, per_dev, sl_count, rows_dev)
    by_owner = jnp.swapaxes(by_owner, 1, 2).reshape(ang_count * sl_count, per_dev * rows_dev)
    owners = ang_count * sl_count
    payload = jnp.concatenate(
        [
            by_owner,
            jnp.broadcast_to(grad_norm, (owners, 1)),
            jnp.broadcast_to(curvature, (owners, 1)),
        ],
        axis=1,
    )
    grad = lax.dot_general(
        stacked, tabs, (((0,), (0,)), ((), ())), precision=lax.Precision.HIGH
    )
    grad = lax.optimization_barrier(grad.reshape(coefficients.shape))
    received = lax.all_to_all(payload, ANG_SL, 0, 0, tiled=True)
    totals = jnp.sum(received, axis=0)
    misfit = totals[: per_dev * rows_dev].reshape(per_dev, rows_dev)
    step_size = totals[per_dev * rows_dev] / (totals[per_dev * rows_dev + 1] + small_eps)
    updated = coefficients - step_size * grad
    return (updated, misfit)


def solution(mesh):
    torus = Mesh(
        mesh.devices.reshape(8, 2, 4, 2, mesh.shape["sl"]),
        ("ang_0", "ang_1", "ang_2", "ang_3", "sl"),
    )
    in_specs = (P(ANG, "sl", None), P(), P(ANG), P(), P(None, None, ANG_SL, None))
    out_specs = (P(None, None, ANG_SL, None), P(ANG, "sl"))
    return jax.shard_map(
        step_body, mesh=torus, in_specs=in_specs, out_specs=out_specs, check_vma=False
    )
```

```python
import math

import jax
import jax.numpy as jnp
from jax import lax
from jax.sharding import Mesh
from jax.sharding import PartitionSpec as P


W = 8192
HALF = 4096
K = 4096
EXTRA = 256
RAMP = 64
ROWS = 8
ANG = ("ang_0", "ang_1", "ang_2", "ang_3")
ANG_SL = ("ang_0", "ang_1", "ang_2", "ang_3", "sl")


paganin_strength = 16.0
small_eps = 1e-06
highest = lax.Precision.HIGHEST


def from_behind(value, axis, steps):
    count = lax.axis_size(axis)
    pairs = [(source, (source + steps) % count) for source in range(count)]
    return lax.ppermute(value, axis, pairs)


def paganin_rows(frequencies):
    row_ids = jnp.arange(ROWS, dtype=jnp.int32)
    row_offset = (row_ids[:, None] - row_ids[None, :]) % ROWS
    cos_table = jnp.cos(
        2.0
        * math.pi
        / ROWS
        * (row_ids[:, None, None] * row_offset[None, :, :] % ROWS).astype(jnp.float32)
    )
    row_freq = jnp.minimum(row_ids, ROWS - row_ids).astype(jnp.float32) / ROWS
    col_freq = frequencies / W
    damping = 1.0 / (
        1.0
        + paganin_strength
        * (col_freq[:, None] * col_freq[:, None] + row_freq[None, :] * row_freq[None, :])
    )
    return jnp.einsum("nq,qij->nij", damping, cos_table, precision=highest) / ROWS


def blend_band(projections, mirrored, offsets):
    position = jnp.arange(EXTRA, dtype=jnp.int32).astype(jnp.float32)
    weight = jnp.clip((position[None, :] - offsets[:, None].astype(jnp.float32)) / RAMP, 0.0, 1.0)
    own_band = projections[:, :, HALF - EXTRA : HALF]
    blended = own_band + weight[:, None, :] * (mirrored - own_band)
    return jnp.concatenate([projections[:, :, : HALF - EXTRA], blended], axis=2)


def spectrum_of(stitched):
    row_count = stitched.shape[0] * stitched.shape[1]
    low_split = W // 128
    outer_count = HALF // low_split
    high_count = K // 128
    folded = stitched.reshape(row_count, outer_count, low_split)
    norm_scale = 1.0 / math.sqrt(HALF)
    outer_ids = jnp.arange(outer_count, dtype=jnp.int32)
    lane_ids = jnp.arange(128, dtype=jnp.int32)
    first_phase = (
        2.0 * math.pi / 128 * (outer_ids[:, None] * lane_ids[None, :] % 128).astype(jnp.float32)
    )
    first_cos = jnp.cos(first_phase) * norm_scale
    first_sin = jnp.sin(first_phase) * norm_scale
    part_real = jnp.einsum("rab,ap->rbp", folded, first_cos, precision=highest)
    part_imag = -jnp.einsum("rab,ap->rbp", folded, first_sin, precision=highest)
    low_ids = jnp.arange(low_split, dtype=jnp.int32)
    twist_phase = 2.0 * math.pi / W * (low_ids[:, None] * lane_ids[None, :]).astype(jnp.float32)
    twist_cos = jnp.cos(twist_phase)
    twist_sin = jnp.sin(twist_phase)
    turned_real = part_real * twist_cos + part_imag * twist_sin
    turned_imag = part_imag * twist_cos - part_real * twist_sin
    high_ids = jnp.arange(high_count, dtype=jnp.int32)
    last_phase = (
        2.0
        * math.pi
        / low_split
        * (low_ids[:, None] * high_ids[None, :] % low_split).astype(jnp.float32)
    )
    last_cos = jnp.cos(last_phase)
    last_sin = jnp.sin(last_phase)
    spec_real = jnp.einsum("rbp,bq->rqp", turned_real, last_cos, precision=highest) + jnp.einsum(
        "rbp,bq->rqp", turned_imag, last_sin, precision=highest
    )
    spec_imag = jnp.einsum("rbp,bq->rqp", turned_imag, last_cos, precision=highest) - jnp.einsum(
        "rbp,bq->rqp", turned_real, last_sin, precision=highest
    )
    return (spec_real, spec_imag)


def step_body(projections, partner, offsets, angles, coefficients):
    ang_count = lax.axis_size(ANG)
    sl_count = lax.axis_size("sl")
    ang_index = lax.axis_index(ANG)
    sl_index = lax.axis_index("sl")
    per_dev = projections.shape[0]
    rows_dev = projections.shape[1]
    total_angles = per_dev * ang_count
    block_freqs = coefficients.shape[2]
    harmonics = coefficients.shape[3]
    columns = ROWS * block_freqs
    own_partners = lax.dynamic_slice_in_dim(partner, ang_index * per_dev, per_dev)
    across_dev = (ang_index + ang_count // 2) % ang_count
    partner_slots = own_partners - across_dev * per_dev
    arrived = from_behind(projections[:, :, HALF:], ANG, ang_count // 2)
    chosen = arrived[0]
    for slot in range(1, per_dev):
        chosen = jnp.where((partner_slots == slot)[:, None, None], arrived[slot], chosen)
    mirrored = jnp.flip(chosen, axis=2)
    stitched = blend_band(projections, mirrored, offsets)
    spec_real, spec_imag = spectrum_of(stitched)
    spectra = jnp.stack([spec_real, spec_imag])
    dev_count = ang_count * sl_count
    lane_split = 128 // block_freqs
    spectra = spectra.reshape(2, per_dev * rows_dev, K // 128, lane_split, block_freqs)
    payload = spectra.transpose(2, 3, 0, 1, 4).reshape(dev_count, -1)
    received = lax.all_to_all(payload, ANG_SL, 0, 0, tiled=True)
    if per_dev == 2 and sl_count == 2:
        half = rows_dev * block_freqs
        row_ids = jnp.arange(dev_count, dtype=jnp.int32)
        lane_ids = jnp.arange(2 * columns, dtype=jnp.int32)
        row_swap = ((row_ids[:, None] ^ 1) == row_ids[None, :]).astype(jnp.float32)
        lane_swap = ((lane_ids[:, None] ^ half) == lane_ids[None, :]).astype(jnp.float32)
        swapped = jnp.dot(
            row_swap, jnp.dot(received, lane_swap, precision=highest), precision=highest
        )
        same_half = (row_ids[:, None] % 2) == ((lane_ids[None, :] // half) % 2)
        own_both = jnp.where(same_half, received, swapped)
    else:
        received = received.reshape(ang_count, sl_count, 2, per_dev, rows_dev * block_freqs)
        own_both = received.transpose(0, 3, 2, 1, 4).reshape(total_angles, 2 * columns)
    freq_base = (ang_index * sl_count + sl_index) * block_freqs
    local_freq = (freq_base + jnp.arange(block_freqs, dtype=jnp.int32)).astype(jnp.float32)
    col_freq = jnp.tile(local_freq, ROWS)
    turn_phase = 2.0 * math.pi / W * col_freq
    turn_cos = jnp.cos(turn_phase)
    turn_sin = jnp.sin(turn_phase)
    own_real = own_both[:, :columns]
    own_imag = own_both[:, columns:]
    swap = (partner[:, None] == jnp.arange(total_angles, dtype=jnp.int32)[None, :]).astype(jnp.float32)
    pair_both = jnp.dot(swap, own_both, precision=highest)
    pair_real = pair_both[:, :columns]
    pair_imag = pair_both[:, columns:]
    comb_real = own_real + turn_cos * pair_real + turn_sin * pair_imag
    comb_imag = own_imag + turn_sin * pair_real - turn_cos * pair_imag
    rows_matrix = paganin_rows(local_freq)
    full_matrix = jnp.einsum(
        "nij,mn->jmin", rows_matrix, jnp.eye(block_freqs, dtype=jnp.float32)
    ).reshape(columns, columns)
    filt_real = jnp.dot(comb_real, full_matrix, precision=highest)
    filt_imag = jnp.dot(comb_imag, full_matrix, precision=highest)
    ramp_weights = (col_freq + 0.5) / K
    coef_rows = coefficients.reshape(2 * columns, harmonics)
    harm_shift = (jnp.arange(harmonics, dtype=jnp.int32) - harmonics // 2).astype(jnp.float32)
    norm_scale = 1.0 / math.sqrt(harmonics)
    phase_tab = angles[:, None] * harm_shift[None, :]
    tabs = jnp.concatenate(
        [jnp.cos(phase_tab) * norm_scale, jnp.sin(phase_tab) * norm_scale]
    )

    def to_image(coef):
        prod = lax.dot_general(
            tabs, coef, (((1,), (1,)), ((), ())), precision=highest
        )
        cos_part, sin_part = prod[:total_angles], prod[total_angles:]
        real = cos_part[:, :columns] - sin_part[:, columns:]
        imag = cos_part[:, columns:] + sin_part[:, :columns]
        return real, imag

    model_real, model_imag = to_image(coef_rows)
    diff_real = model_real - filt_real
    diff_imag = model_imag - filt_imag
    resid_real = ramp_weights * diff_real
    resid_imag = ramp_weights * diff_imag
    energy = (diff_real * resid_real + diff_imag * resid_imag).reshape(
        total_angles, ROWS, block_freqs
    )
    misfit_table = jnp.sum(energy, axis=2) / K
    stacked = jnp.concatenate(
        [
            jnp.concatenate([resid_real, resid_imag], axis=1),
            jnp.concatenate([resid_imag, -resid_real], axis=1),
        ]
    )
    gram = lax.dot_general(tabs, tabs, (((1,), (1,)), ((), ())), precision=highest)
    gram_real = gram[:total_angles, :total_angles] + gram[total_angles:, total_angles:]
    gram_imag = gram[total_angles:, :total_angles] - gram[:total_angles, total_angles:]
    gram_both = jnp.concatenate(
        [
            jnp.concatenate([gram_real, -gram_imag], axis=1),
            jnp.concatenate([gram_imag, gram_real], axis=1),
        ]
    )
    resid_both = jnp.concatenate([resid_real, resid_imag])
    image_both = jnp.dot(gram_both, resid_both, precision=lax.Precision.HIGH)
    image_real, image_imag = image_both[:total_angles], image_both[total_angles:]
    curvature = jnp.sum(ramp_weights * (image_real * image_real + image_imag * image_imag))
    grad_norm = jnp.sum(resid_real * image_real + resid_imag * image_imag)
    by_owner = misfit_table.reshape(ang_count, per_dev, sl_count, rows_dev)
    by_owner = jnp.swapaxes(by_owner, 1, 2).reshape(ang_count * sl_count, per_dev * rows_dev)
    scalars = jnp.broadcast_to(jnp.stack([grad_norm, curvature])[None], (ang_count * sl_count, 2))
    payload = jnp.concatenate([by_owner, scalars], axis=1)
    received = lax.all_to_all(payload, ANG_SL, 0, 0, tiled=True)
    totals = jnp.sum(received, axis=0)
    misfit = totals[: per_dev * rows_dev].reshape(per_dev, rows_dev)
    step_size = totals[per_dev * rows_dev] / (totals[per_dev * rows_dev + 1] + small_eps)
    step_grad = lax.dot_general(
        -step_size * stacked, tabs, (((0,), (0,)), ((), ())), precision=lax.Precision.HIGH
    )
    updated = coefficients + step_grad.reshape(coefficients.shape)
    return (updated, misfit)


def solution(mesh):
    torus = Mesh(
        mesh.devices.reshape(8, 2, 4, 2, mesh.shape["sl"]),
        ("ang_0", "ang_1", "ang_2", "ang_3", "sl"),
    )
    in_specs = (P(ANG, "sl", None), P(), P(ANG), P(), P(None, None, ANG_SL, None))
    out_specs = (P(None, None, ANG_SL, None), P(ANG, "sl"))
    return jax.shard_map(
        step_body, mesh=torus, in_specs=in_specs, out_specs=out_specs, check_vma=False
    )
```

```python
import math

import jax
import jax.numpy as jnp
from jax import lax
from jax.sharding import Mesh
from jax.sharding import PartitionSpec as P


W = 8192
HALF = 4096
K = 4096
EXTRA = 256
RAMP = 64
ROWS = 8
ANG = ("ang_0", "ang_1", "ang_2", "ang_3")
ANG_SL = ("ang_0", "ang_1", "ang_2", "ang_3", "sl")


paganin_strength = 16.0
small_eps = 1e-06
highest = lax.Precision.HIGHEST


def from_behind(value, axis, steps):
    count = lax.axis_size(axis)
    pairs = [(source, (source + steps) % count) for source in range(count)]
    return lax.ppermute(value, axis, pairs)


def paganin_rows(frequencies):
    row_ids = jnp.arange(ROWS, dtype=jnp.int32)
    row_offset = (row_ids[:, None] - row_ids[None, :]) % ROWS
    cos_table = jnp.cos(
        2.0
        * math.pi
        / ROWS
        * (row_ids[:, None, None] * row_offset[None, :, :] % ROWS).astype(jnp.float32)
    )
    row_freq = jnp.minimum(row_ids, ROWS - row_ids).astype(jnp.float32) / ROWS
    col_freq = frequencies / W
    damping = 1.0 / (
        1.0
        + paganin_strength
        * (col_freq[:, None] * col_freq[:, None] + row_freq[None, :] * row_freq[None, :])
    )
    return jnp.einsum("nq,qij->nij", damping, cos_table, precision=highest) / ROWS


def blend_band(projections, mirrored, offsets):
    position = jnp.arange(EXTRA, dtype=jnp.int32).astype(jnp.float32)
    weight = jnp.clip((position[None, :] - offsets[:, None].astype(jnp.float32)) / RAMP, 0.0, 1.0)
    own_band = projections[:, :, HALF - EXTRA : HALF]
    blended = own_band + weight[:, None, :] * (mirrored - own_band)
    return jnp.concatenate([projections[:, :, : HALF - EXTRA], blended], axis=2)


def spectrum_of(stitched):
    row_count = stitched.shape[0] * stitched.shape[1]
    low_split = W // 128
    outer_count = HALF // low_split
    high_count = K // 128
    folded = stitched.reshape(row_count, outer_count, low_split)
    norm_scale = 1.0 / math.sqrt(HALF)
    outer_ids = jnp.arange(outer_count, dtype=jnp.int32)
    lane_ids = jnp.arange(128, dtype=jnp.int32)
    first_phase = (
        2.0 * math.pi / 128 * (outer_ids[:, None] * lane_ids[None, :] % 128).astype(jnp.float32)
    )
    first_cos = jnp.cos(first_phase) * norm_scale
    first_sin = jnp.sin(first_phase) * norm_scale
    part_real = jnp.einsum("rab,ap->rbp", folded, first_cos, precision=highest)
    part_imag = -jnp.einsum("rab,ap->rbp", folded, first_sin, precision=highest)
    low_ids = jnp.arange(low_split, dtype=jnp.int32)
    twist_phase = 2.0 * math.pi / W * (low_ids[:, None] * lane_ids[None, :]).astype(jnp.float32)
    twist_cos = jnp.cos(twist_phase)
    twist_sin = jnp.sin(twist_phase)
    turned_real = part_real * twist_cos + part_imag * twist_sin
    turned_imag = part_imag * twist_cos - part_real * twist_sin
    high_ids = jnp.arange(high_count, dtype=jnp.int32)
    last_phase = (
        2.0
        * math.pi
        / low_split
        * (low_ids[:, None] * high_ids[None, :] % low_split).astype(jnp.float32)
    )
    last_cos = jnp.cos(last_phase)
    last_sin = jnp.sin(last_phase)
    spec_real = jnp.einsum("rbp,bq->rqp", turned_real, last_cos, precision=highest) + jnp.einsum(
        "rbp,bq->rqp", turned_imag, last_sin, precision=highest
    )
    spec_imag = jnp.einsum("rbp,bq->rqp", turned_imag, last_cos, precision=highest) - jnp.einsum(
        "rbp,bq->rqp", turned_real, last_sin, precision=highest
    )
    return (spec_real, spec_imag)


def step_body(projections, partner, offsets, angles, coefficients):
    ang_count = lax.axis_size(ANG)
    sl_count = lax.axis_size("sl")
    ang_index = lax.axis_index(ANG)
    sl_index = lax.axis_index("sl")
    per_dev = projections.shape[0]
    rows_dev = projections.shape[1]
    total_angles = per_dev * ang_count
    block_freqs = coefficients.shape[2]
    harmonics = coefficients.shape[3]
    columns = ROWS * block_freqs
    own_partners = lax.dynamic_slice_in_dim(partner, ang_index * per_dev, per_dev)
    across_dev = (ang_index + ang_count // 2) % ang_count
    partner_slots = own_partners - across_dev * per_dev
    arrived = from_behind(projections, ANG, ang_count // 2)[:, :, HALF:]
    chosen = arrived[0]
    for slot in range(1, per_dev):
        chosen = jnp.where((partner_slots == slot)[:, None, None], arrived[slot], chosen)
    mirrored = jnp.flip(chosen, axis=2)
    stitched = blend_band(projections, mirrored, offsets)
    spec_real, spec_imag = spectrum_of(stitched)
    spectra = jnp.stack([spec_real, spec_imag])
    dev_count = ang_count * sl_count
    lane_split = 128 // block_freqs
    spectra = spectra.reshape(2, per_dev * rows_dev, K // 128, lane_split, block_freqs)
    payload = spectra.transpose(2, 3, 0, 1, 4).reshape(dev_count, -1)
    received = lax.all_to_all(payload, ANG_SL, 0, 0, tiled=True)
    if per_dev == 2 and sl_count == 2:
        half = rows_dev * block_freqs
        row_ids = jnp.arange(dev_count, dtype=jnp.int32)
        lane_ids = jnp.arange(2 * columns, dtype=jnp.int32)
        row_swap = ((row_ids[:, None] ^ 1) == row_ids[None, :]).astype(jnp.float32)
        lane_swap = ((lane_ids[:, None] ^ half) == lane_ids[None, :]).astype(jnp.float32)
        swapped = jnp.dot(
            row_swap, jnp.dot(received, lane_swap, precision=highest), precision=highest
        )
        same_half = (row_ids[:, None] % 2) == ((lane_ids[None, :] // half) % 2)
        own_both = jnp.where(same_half, received, swapped)
    else:
        received = received.reshape(ang_count, sl_count, 2, per_dev, rows_dev * block_freqs)
        own_both = received.transpose(0, 3, 2, 1, 4).reshape(total_angles, 2 * columns)
    freq_base = (ang_index * sl_count + sl_index) * block_freqs
    local_freq = (freq_base + jnp.arange(block_freqs, dtype=jnp.int32)).astype(jnp.float32)
    col_freq = jnp.tile(local_freq, ROWS)
    turn_phase = 2.0 * math.pi / W * col_freq
    turn_cos = jnp.cos(turn_phase)
    turn_sin = jnp.sin(turn_phase)
    own_real = own_both[:, :columns]
    own_imag = own_both[:, columns:]
    swap = (partner[:, None] == jnp.arange(total_angles, dtype=jnp.int32)[None, :]).astype(jnp.float32)
    pair_both = jnp.dot(swap, own_both, precision=highest)
    pair_real = pair_both[:, :columns]
    pair_imag = pair_both[:, columns:]
    comb_real = own_real + turn_cos * pair_real + turn_sin * pair_imag
    comb_imag = own_imag + turn_sin * pair_real - turn_cos * pair_imag
    rows_matrix = paganin_rows(local_freq)
    full_matrix = jnp.einsum(
        "nij,mn->jmin", rows_matrix, jnp.eye(block_freqs, dtype=jnp.float32)
    ).reshape(columns, columns)
    filt_real = jnp.dot(comb_real, full_matrix, precision=highest)
    filt_imag = jnp.dot(comb_imag, full_matrix, precision=highest)
    ramp_weights = (col_freq + 0.5) / K
    coef_rows = coefficients.reshape(2 * columns, harmonics)
    harm_shift = (jnp.arange(harmonics, dtype=jnp.int32) - harmonics // 2).astype(jnp.float32)
    norm_scale = 1.0 / math.sqrt(harmonics)
    phase_tab = angles[:, None] * harm_shift[None, :]
    tabs = jnp.concatenate(
        [jnp.cos(phase_tab) * norm_scale, jnp.sin(phase_tab) * norm_scale]
    )

    def to_image(coef):
        prod = lax.dot_general(
            tabs, coef, (((1,), (1,)), ((), ())), precision=highest
        )
        cos_part, sin_part = prod[:total_angles], prod[total_angles:]
        real = cos_part[:, :columns] - sin_part[:, columns:]
        imag = cos_part[:, columns:] + sin_part[:, :columns]
        return real, imag

    model_real, model_imag = to_image(coef_rows)
    diff_real = model_real - filt_real
    diff_imag = model_imag - filt_imag
    resid_real = ramp_weights * diff_real
    resid_imag = ramp_weights * diff_imag
    energy = (diff_real * resid_real + diff_imag * resid_imag).reshape(
        total_angles, ROWS, block_freqs
    )
    misfit_table = jnp.sum(energy, axis=2) / K
    stacked = jnp.concatenate(
        [
            jnp.concatenate([resid_real, resid_imag], axis=1),
            jnp.concatenate([resid_imag, -resid_real], axis=1),
        ]
    )
    gram = lax.dot_general(tabs, tabs, (((1,), (1,)), ((), ())), precision=highest)
    gram_real = gram[:total_angles, :total_angles] + gram[total_angles:, total_angles:]
    gram_imag = gram[total_angles:, :total_angles] - gram[:total_angles, total_angles:]
    gram_both = jnp.concatenate(
        [
            jnp.concatenate([gram_real, -gram_imag], axis=1),
            jnp.concatenate([gram_imag, gram_real], axis=1),
        ]
    )
    resid_both = jnp.concatenate([resid_real, resid_imag])
    image_both = jnp.dot(gram_both, resid_both, precision=lax.Precision.HIGH)
    image_real, image_imag = image_both[:total_angles], image_both[total_angles:]
    owners = ang_count * sl_count
    if per_dev == 2 and sl_count == 2:
        cells = jnp.concatenate(
            [
                diff_real * resid_real + diff_imag * resid_imag,
                resid_real * image_real + resid_imag * image_imag,
                ramp_weights * (image_real * image_real + image_imag * image_imag),
            ],
            axis=1,
        )
        cell_ids = jnp.arange(3 * columns, dtype=jnp.int32)
        out_ids = jnp.arange(ROWS + 2, dtype=jnp.int32)
        target = jnp.where(
            cell_ids < columns, cell_ids // block_freqs, ROWS + cell_ids // columns - 1
        )
        scale = jnp.where(cell_ids < columns, 1.0 / K, 1.0).astype(jnp.float32)
        summing = jnp.where(target[:, None] == out_ids[None, :], scale[:, None], 0.0)
        sums = jnp.dot(cells, summing, precision=highest)
        table = sums[:, :ROWS]
        row_ids = jnp.arange(owners, dtype=jnp.int32)
        lane_ids = jnp.arange(ROWS, dtype=jnp.int32)
        row_swap = ((row_ids[:, None] ^ 1) == row_ids[None, :]).astype(jnp.float32)
        lane_swap = ((lane_ids[:, None] ^ rows_dev) == lane_ids[None, :]).astype(jnp.float32)
        swapped = jnp.dot(
            row_swap, jnp.dot(table, lane_swap, precision=highest), precision=highest
        )
        same_half = (row_ids[:, None] % 2) == ((lane_ids[None, :] // rows_dev) % 2)
        by_owner = jnp.where(same_half, table, swapped)
        spread = jnp.ones((owners, total_angles), jnp.float32)
        scalars = jnp.dot(spread, sums[:, ROWS:], precision=highest)
    else:
        curvature = jnp.sum(ramp_weights * (image_real * image_real + image_imag * image_imag))
        grad_norm = jnp.sum(resid_real * image_real + resid_imag * image_imag)
        by_owner = misfit_table.reshape(ang_count, per_dev, sl_count, rows_dev)
        by_owner = jnp.swapaxes(by_owner, 1, 2).reshape(owners, per_dev * rows_dev)
        scalars = jnp.broadcast_to(jnp.stack([grad_norm, curvature])[None], (owners, 2))
    payload = jnp.concatenate([by_owner, scalars], axis=1)
    received = lax.all_to_all(payload, ANG_SL, 0, 0, tiled=True)
    totals = jnp.sum(received, axis=0)
    misfit = totals[: per_dev * rows_dev].reshape(per_dev, rows_dev)
    step_size = totals[per_dev * rows_dev] / (totals[per_dev * rows_dev + 1] + small_eps)
    step_grad = lax.dot_general(
        -step_size * stacked, tabs, (((0,), (0,)), ((), ())), precision=lax.Precision.HIGH
    )
    updated = coefficients + step_grad.reshape(coefficients.shape)
    return (updated, misfit)


def solution(mesh):
    torus = Mesh(
        mesh.devices.reshape(8, 2, 4, 2, mesh.shape["sl"]),
        ("ang_0", "ang_1", "ang_2", "ang_3", "sl"),
    )
    in_specs = (P(ANG, "sl", None), P(), P(ANG), P(), P(None, None, ANG_SL, None))
    out_specs = (P(None, None, ANG_SL, None), P(ANG, "sl"))
    return jax.shard_map(
        step_body, mesh=torus, in_specs=in_specs, out_specs=out_specs, check_vma=False
    )
```

```python
import math

import jax
import jax.numpy as jnp
from jax import lax
from jax.sharding import Mesh
from jax.sharding import PartitionSpec as P


W = 8192
HALF = 4096
K = 4096
EXTRA = 256
RAMP = 64
ROWS = 8
ANG = ("ang_0", "ang_1", "ang_2", "ang_3")
ANG_SL = ("ang_0", "ang_1", "ang_2", "ang_3", "sl")


paganin_strength = 16.0
small_eps = 1e-06
highest = lax.Precision.HIGHEST


def from_behind(value, axis, steps):
    count = lax.axis_size(axis)
    pairs = [(source, (source + steps) % count) for source in range(count)]
    return lax.ppermute(value, axis, pairs)


def paganin_rows(frequencies):
    row_ids = jnp.arange(ROWS, dtype=jnp.int32)
    row_offset = (row_ids[:, None] - row_ids[None, :]) % ROWS
    cos_table = jnp.cos(
        2.0
        * math.pi
        / ROWS
        * (row_ids[:, None, None] * row_offset[None, :, :] % ROWS).astype(jnp.float32)
    )
    row_freq = jnp.minimum(row_ids, ROWS - row_ids).astype(jnp.float32) / ROWS
    col_freq = frequencies / W
    damping = 1.0 / (
        1.0
        + paganin_strength
        * (col_freq[:, None] * col_freq[:, None] + row_freq[None, :] * row_freq[None, :])
    )
    return jnp.einsum("nq,qij->nij", damping, cos_table, precision=highest) / ROWS


def blend_band(projections, mirrored, offsets):
    position = jnp.arange(EXTRA, dtype=jnp.int32).astype(jnp.float32)
    weight = jnp.clip((position[None, :] - offsets[:, None].astype(jnp.float32)) / RAMP, 0.0, 1.0)
    own_band = projections[:, :, HALF - EXTRA : HALF]
    blended = own_band + weight[:, None, :] * (mirrored - own_band)
    return jnp.concatenate([projections[:, :, : HALF - EXTRA], blended], axis=2)


def spectrum_of(stitched):
    row_count = stitched.shape[0] * stitched.shape[1]
    low_split = W // 128
    outer_count = HALF // low_split
    high_count = K // 128
    folded = stitched.reshape(row_count, outer_count, low_split)
    norm_scale = 1.0 / math.sqrt(HALF)
    outer_ids = jnp.arange(outer_count, dtype=jnp.int32)
    lane_ids = jnp.arange(128, dtype=jnp.int32)
    first_phase = (
        2.0 * math.pi / 128 * (outer_ids[:, None] * lane_ids[None, :] % 128).astype(jnp.float32)
    )
    first_cos = jnp.cos(first_phase) * norm_scale
    first_sin = jnp.sin(first_phase) * norm_scale
    first_both = jnp.concatenate([first_cos, -first_sin], axis=1)
    part = jnp.einsum("rab,ap->rbp", folded, first_both, precision=highest)
    part_real, part_imag = part[:, :, :128], part[:, :, 128:]
    low_ids = jnp.arange(low_split, dtype=jnp.int32)
    twist_phase = 2.0 * math.pi / W * (low_ids[:, None] * lane_ids[None, :]).astype(jnp.float32)
    twist_cos = jnp.cos(twist_phase)
    twist_sin = jnp.sin(twist_phase)
    turned_real = part_real * twist_cos + part_imag * twist_sin
    turned_imag = part_imag * twist_cos - part_real * twist_sin
    high_ids = jnp.arange(high_count, dtype=jnp.int32)
    last_phase = (
        2.0
        * math.pi
        / low_split
        * (low_ids[:, None] * high_ids[None, :] % low_split).astype(jnp.float32)
    )
    last_cos = jnp.cos(last_phase)
    last_sin = jnp.sin(last_phase)
    turned = jnp.concatenate([turned_real, turned_imag], axis=1)
    last_both = jnp.concatenate(
        [
            jnp.concatenate([last_cos, -last_sin], axis=1),
            jnp.concatenate([last_sin, last_cos], axis=1),
        ]
    )
    spec = jnp.einsum("rbp,bq->rqp", turned, last_both, precision=highest)
    spec_real, spec_imag = spec[:, :high_count], spec[:, high_count:]
    return (spec_real, spec_imag)


def step_body(projections, partner, offsets, angles, coefficients):
    ang_count = lax.axis_size(ANG)
    sl_count = lax.axis_size("sl")
    ang_index = lax.axis_index(ANG)
    sl_index = lax.axis_index("sl")
    per_dev = projections.shape[0]
    rows_dev = projections.shape[1]
    total_angles = per_dev * ang_count
    block_freqs = coefficients.shape[2]
    harmonics = coefficients.shape[3]
    columns = ROWS * block_freqs
    own_partners = lax.dynamic_slice_in_dim(partner, ang_index * per_dev, per_dev)
    across_dev = (ang_index + ang_count // 2) % ang_count
    partner_slots = own_partners - across_dev * per_dev
    arrived = from_behind(projections[:, :, HALF:], ANG, ang_count // 2)
    chosen = arrived[0]
    for slot in range(1, per_dev):
        chosen = jnp.where((partner_slots == slot)[:, None, None], arrived[slot], chosen)
    mirrored = jnp.flip(chosen, axis=2)
    stitched = blend_band(projections, mirrored, offsets)
    spec_real, spec_imag = spectrum_of(stitched)
    spectra = jnp.stack([spec_real, spec_imag])
    dev_count = ang_count * sl_count
    lane_split = 128 // block_freqs
    spectra = spectra.reshape(2, per_dev * rows_dev, K // 128, lane_split, block_freqs)
    payload = spectra.transpose(2, 3, 0, 1, 4).reshape(dev_count, -1)
    received = lax.all_to_all(payload, ANG_SL, 0, 0, tiled=True)
    if per_dev == 2 and sl_count == 2:
        half = rows_dev * block_freqs
        row_ids = jnp.arange(dev_count, dtype=jnp.int32)
        lane_ids = jnp.arange(2 * columns, dtype=jnp.int32)
        row_swap = ((row_ids[:, None] ^ 1) == row_ids[None, :]).astype(jnp.float32)
        lane_swap = ((lane_ids[:, None] ^ half) == lane_ids[None, :]).astype(jnp.float32)
        swapped = jnp.dot(
            row_swap, jnp.dot(received, lane_swap, precision=highest), precision=highest
        )
        same_half = (row_ids[:, None] % 2) == ((lane_ids[None, :] // half) % 2)
        own_both = jnp.where(same_half, received, swapped)
    else:
        received = received.reshape(ang_count, sl_count, 2, per_dev, rows_dev * block_freqs)
        own_both = received.transpose(0, 3, 2, 1, 4).reshape(total_angles, 2 * columns)
    freq_base = (ang_index * sl_count + sl_index) * block_freqs
    local_freq = (freq_base + jnp.arange(block_freqs, dtype=jnp.int32)).astype(jnp.float32)
    col_freq = jnp.tile(local_freq, ROWS)
    turn_phase = 2.0 * math.pi / W * col_freq
    turn_cos = jnp.cos(turn_phase)
    turn_sin = jnp.sin(turn_phase)
    own_real = own_both[:, :columns]
    own_imag = own_both[:, columns:]
    swap = (partner[:, None] == jnp.arange(total_angles, dtype=jnp.int32)[None, :]).astype(jnp.float32)
    pair_both = jnp.dot(swap, own_both, precision=highest)
    pair_real = pair_both[:, :columns]
    pair_imag = pair_both[:, columns:]
    comb_real = own_real + turn_cos * pair_real + turn_sin * pair_imag
    comb_imag = own_imag + turn_sin * pair_real - turn_cos * pair_imag
    rows_matrix = paganin_rows(local_freq)
    full_matrix = jnp.einsum(
        "nij,mn->jmin", rows_matrix, jnp.eye(block_freqs, dtype=jnp.float32)
    ).reshape(columns, columns)
    filt_real = jnp.dot(comb_real, full_matrix, precision=highest)
    filt_imag = jnp.dot(comb_imag, full_matrix, precision=highest)
    ramp_weights = (col_freq + 0.5) / K
    coef_rows = coefficients.reshape(2 * columns, harmonics)
    harm_shift = (jnp.arange(harmonics, dtype=jnp.int32) - harmonics // 2).astype(jnp.float32)
    norm_scale = 1.0 / math.sqrt(harmonics)
    phase_tab = angles[:, None] * harm_shift[None, :]
    tabs = jnp.concatenate(
        [jnp.cos(phase_tab) * norm_scale, jnp.sin(phase_tab) * norm_scale]
    )

    def to_image(coef):
        prod = lax.dot_general(
            tabs, coef, (((1,), (1,)), ((), ())), precision=highest
        )
        cos_part, sin_part = prod[:total_angles], prod[total_angles:]
        real = cos_part[:, :columns] - sin_part[:, columns:]
        imag = cos_part[:, columns:] + sin_part[:, :columns]
        return real, imag

    model_real, model_imag = to_image(coef_rows)
    diff_real = model_real - filt_real
    diff_imag = model_imag - filt_imag
    resid_real = ramp_weights * diff_real
    resid_imag = ramp_weights * diff_imag
    energy = (diff_real * resid_real + diff_imag * resid_imag).reshape(
        total_angles, ROWS, block_freqs
    )
    misfit_table = jnp.sum(energy, axis=2) / K
    stacked = jnp.concatenate(
        [
            jnp.concatenate([resid_real, resid_imag], axis=1),
            jnp.concatenate([resid_imag, -resid_real], axis=1),
        ]
    )
    gram = lax.dot_general(tabs, tabs, (((1,), (1,)), ((), ())), precision=highest)
    gram_real = gram[:total_angles, :total_angles] + gram[total_angles:, total_angles:]
    gram_imag = gram[total_angles:, :total_angles] - gram[:total_angles, total_angles:]
    gram_both = jnp.concatenate(
        [
            jnp.concatenate([gram_real, -gram_imag], axis=1),
            jnp.concatenate([gram_imag, gram_real], axis=1),
        ]
    )
    resid_both = jnp.concatenate([resid_real, resid_imag])
    image_both = jnp.dot(gram_both, resid_both, precision=lax.Precision.HIGH)
    image_real, image_imag = image_both[:total_angles], image_both[total_angles:]
    owners = ang_count * sl_count
    if per_dev == 2 and sl_count == 2:
        cells = jnp.concatenate(
            [
                diff_real * resid_real + diff_imag * resid_imag,
                resid_real * image_real + resid_imag * image_imag,
                ramp_weights * (image_real * image_real + image_imag * image_imag),
            ],
            axis=1,
        )
        cell_ids = jnp.arange(3 * columns, dtype=jnp.int32)
        out_ids = jnp.arange(ROWS + 2, dtype=jnp.int32)
        target = jnp.where(
            cell_ids < columns, cell_ids // block_freqs, ROWS + cell_ids // columns - 1
        )
        scale = jnp.where(cell_ids < columns, 1.0 / K, 1.0).astype(jnp.float32)
        summing = jnp.where(target[:, None] == out_ids[None, :], scale[:, None], 0.0)
        sums = jnp.dot(cells, summing, precision=highest)
        table = sums[:, :ROWS]
        row_ids = jnp.arange(owners, dtype=jnp.int32)
        lane_ids = jnp.arange(ROWS, dtype=jnp.int32)
        row_swap = ((row_ids[:, None] ^ 1) == row_ids[None, :]).astype(jnp.float32)
        lane_swap = ((lane_ids[:, None] ^ rows_dev) == lane_ids[None, :]).astype(jnp.float32)
        swapped = jnp.dot(
            row_swap, jnp.dot(table, lane_swap, precision=highest), precision=highest
        )
        same_half = (row_ids[:, None] % 2) == ((lane_ids[None, :] // rows_dev) % 2)
        by_owner = jnp.where(same_half, table, swapped)
        spread = jnp.ones((owners, total_angles), jnp.float32)
        scalars = jnp.dot(spread, sums[:, ROWS:], precision=highest)
    else:
        curvature = jnp.sum(ramp_weights * (image_real * image_real + image_imag * image_imag))
        grad_norm = jnp.sum(resid_real * image_real + resid_imag * image_imag)
        by_owner = misfit_table.reshape(ang_count, per_dev, sl_count, rows_dev)
        by_owner = jnp.swapaxes(by_owner, 1, 2).reshape(owners, per_dev * rows_dev)
        scalars = jnp.broadcast_to(jnp.stack([grad_norm, curvature])[None], (owners, 2))
    payload = jnp.concatenate([by_owner, scalars], axis=1)
    received = lax.all_to_all(payload, ANG_SL, 0, 0, tiled=True)
    totals = jnp.sum(received, axis=0)
    misfit = totals[: per_dev * rows_dev].reshape(per_dev, rows_dev)
    step_size = totals[per_dev * rows_dev] / (totals[per_dev * rows_dev + 1] + small_eps)
    step_grad = lax.dot_general(
        -step_size * stacked, tabs, (((0,), (0,)), ((), ())), precision=lax.Precision.HIGH
    )
    updated = (coef_rows + step_grad).reshape(coefficients.shape)
    return (updated, misfit)


def solution(mesh):
    torus = Mesh(
        mesh.devices.reshape(8, 2, 4, 2, mesh.shape["sl"]),
        ("ang_0", "ang_1", "ang_2", "ang_3", "sl"),
    )
    in_specs = (P(ANG, "sl", None), P(), P(ANG), P(), P(None, None, ANG_SL, None))
    out_specs = (P(None, None, ANG_SL, None), P(ANG, "sl"))
    return jax.shard_map(
        step_body, mesh=torus, in_specs=in_specs, out_specs=out_specs, check_vma=False
    )
```

```python
import math

import jax
import jax.numpy as jnp
from jax import lax
from jax.sharding import Mesh
from jax.sharding import PartitionSpec as P


W = 8192
HALF = 4096
K = 4096
EXTRA = 256
RAMP = 64
ROWS = 8
ANG = ("ang_0", "ang_1", "ang_2", "ang_3")
ANG_SL = ("ang_0", "ang_1", "ang_2", "ang_3", "sl")


paganin_strength = 16.0
small_eps = 1e-06
highest = lax.Precision.HIGHEST


def from_behind(value, axis, steps):
    count = lax.axis_size(axis)
    pairs = [(source, (source + steps) % count) for source in range(count)]
    return lax.ppermute(value, axis, pairs)


def paganin_rows(frequencies):
    row_ids = jnp.arange(ROWS, dtype=jnp.int32)
    row_offset = (row_ids[:, None] - row_ids[None, :]) % ROWS
    cos_table = jnp.cos(
        2.0
        * math.pi
        / ROWS
        * (row_ids[:, None, None] * row_offset[None, :, :] % ROWS).astype(jnp.float32)
    )
    row_freq = jnp.minimum(row_ids, ROWS - row_ids).astype(jnp.float32) / ROWS
    col_freq = frequencies / W
    damping = 1.0 / (
        1.0
        + paganin_strength
        * (col_freq[:, None] * col_freq[:, None] + row_freq[None, :] * row_freq[None, :])
    )
    return jnp.einsum("nq,qij->nij", damping, cos_table, precision=highest) / ROWS


def blend_band(projections, mirrored, offsets):
    position = jnp.arange(EXTRA, dtype=jnp.int32).astype(jnp.float32)
    weight = jnp.clip((position[None, :] - offsets[:, None].astype(jnp.float32)) / RAMP, 0.0, 1.0)
    own_band = projections[:, :, HALF - EXTRA : HALF]
    blended = own_band + weight[:, None, :] * (mirrored - own_band)
    return jnp.concatenate([projections[:, :, : HALF - EXTRA], blended], axis=2)


def spectrum_of(stitched):
    row_count = stitched.shape[0] * stitched.shape[1]
    low_split = W // 128
    outer_count = HALF // low_split
    high_count = K // 128
    folded = stitched.reshape(row_count, outer_count, low_split)
    norm_scale = 1.0 / math.sqrt(HALF)
    outer_ids = jnp.arange(outer_count, dtype=jnp.int32)
    lane_ids = jnp.arange(128, dtype=jnp.int32)
    first_phase = (
        2.0 * math.pi / 128 * (outer_ids[:, None] * lane_ids[None, :] % 128).astype(jnp.float32)
    )
    first_cos = jnp.cos(first_phase) * norm_scale
    first_sin = jnp.sin(first_phase) * norm_scale
    first_both = jnp.concatenate([first_cos, -first_sin], axis=1)
    part = jnp.einsum("rab,ap->rbp", folded, first_both, precision=lax.Precision.HIGH)
    part_real, part_imag = part[:, :, :128], part[:, :, 128:]
    low_ids = jnp.arange(low_split, dtype=jnp.int32)
    twist_phase = 2.0 * math.pi / W * (low_ids[:, None] * lane_ids[None, :]).astype(jnp.float32)
    twist_cos = jnp.cos(twist_phase)
    twist_sin = jnp.sin(twist_phase)
    turned_real = part_real * twist_cos + part_imag * twist_sin
    turned_imag = part_imag * twist_cos - part_real * twist_sin
    high_ids = jnp.arange(high_count, dtype=jnp.int32)
    last_phase = (
        2.0
        * math.pi
        / low_split
        * (low_ids[:, None] * high_ids[None, :] % low_split).astype(jnp.float32)
    )
    last_cos = jnp.cos(last_phase)
    last_sin = jnp.sin(last_phase)
    turned = jnp.concatenate([turned_real, turned_imag], axis=1)
    last_both = jnp.concatenate(
        [
            jnp.concatenate([last_cos, -last_sin], axis=1),
            jnp.concatenate([last_sin, last_cos], axis=1),
        ]
    )
    spec = jnp.einsum("rbp,bq->rqp", turned, last_both, precision=lax.Precision.HIGH)
    spec_real, spec_imag = spec[:, :high_count], spec[:, high_count:]
    return (spec_real, spec_imag)


def step_body(projections, partner, offsets, angles, coefficients):
    ang_count = lax.axis_size(ANG)
    sl_count = lax.axis_size("sl")
    ang_index = lax.axis_index(ANG)
    sl_index = lax.axis_index("sl")
    per_dev = projections.shape[0]
    rows_dev = projections.shape[1]
    total_angles = per_dev * ang_count
    block_freqs = coefficients.shape[2]
    harmonics = coefficients.shape[3]
    columns = ROWS * block_freqs
    own_partners = lax.dynamic_slice_in_dim(partner, ang_index * per_dev, per_dev)
    across_dev = (ang_index + ang_count // 2) % ang_count
    partner_slots = own_partners - across_dev * per_dev
    arrived = from_behind(projections[:, :, HALF:], ANG, ang_count // 2)
    chosen = arrived[0]
    for slot in range(1, per_dev):
        chosen = jnp.where((partner_slots == slot)[:, None, None], arrived[slot], chosen)
    mirrored = jnp.flip(chosen, axis=2)
    stitched = blend_band(projections, mirrored, offsets)
    spec_real, spec_imag = spectrum_of(stitched)
    spectra = jnp.stack([spec_real, spec_imag])
    dev_count = ang_count * sl_count
    lane_split = 128 // block_freqs
    spectra = spectra.reshape(2, per_dev * rows_dev, K // 128, lane_split, block_freqs)
    payload = spectra.transpose(2, 3, 0, 1, 4).reshape(dev_count, -1)
    received = lax.all_to_all(payload, ANG_SL, 0, 0, tiled=True)
    if per_dev == 2 and sl_count == 2:
        half = rows_dev * block_freqs
        row_ids = jnp.arange(dev_count, dtype=jnp.int32)
        lane_ids = jnp.arange(2 * columns, dtype=jnp.int32)
        row_swap = ((row_ids[:, None] ^ 1) == row_ids[None, :]).astype(jnp.float32)
        lane_swap = ((lane_ids[:, None] ^ half) == lane_ids[None, :]).astype(jnp.float32)
        swapped = jnp.dot(
            row_swap, jnp.dot(received, lane_swap, precision=highest), precision=highest
        )
        same_half = (row_ids[:, None] % 2) == ((lane_ids[None, :] // half) % 2)
        own_both = jnp.where(same_half, received, swapped)
    else:
        received = received.reshape(ang_count, sl_count, 2, per_dev, rows_dev * block_freqs)
        own_both = received.transpose(0, 3, 2, 1, 4).reshape(total_angles, 2 * columns)
    freq_base = (ang_index * sl_count + sl_index) * block_freqs
    local_freq = (freq_base + jnp.arange(block_freqs, dtype=jnp.int32)).astype(jnp.float32)
    col_freq = jnp.tile(local_freq, ROWS)
    turn_phase = 2.0 * math.pi / W * col_freq
    turn_cos = jnp.cos(turn_phase)
    turn_sin = jnp.sin(turn_phase)
    own_real = own_both[:, :columns]
    own_imag = own_both[:, columns:]
    swap = (partner[:, None] == jnp.arange(total_angles, dtype=jnp.int32)[None, :]).astype(jnp.float32)
    pair_both = jnp.dot(swap, own_both, precision=highest)
    pair_real = pair_both[:, :columns]
    pair_imag = pair_both[:, columns:]
    comb_real = own_real + turn_cos * pair_real + turn_sin * pair_imag
    comb_imag = own_imag + turn_sin * pair_real - turn_cos * pair_imag
    rows_matrix = paganin_rows(local_freq)
    full_matrix = jnp.einsum(
        "nij,mn->jmin", rows_matrix, jnp.eye(block_freqs, dtype=jnp.float32)
    ).reshape(columns, columns)
    filt_real = jnp.dot(comb_real, full_matrix, precision=highest)
    filt_imag = jnp.dot(comb_imag, full_matrix, precision=highest)
    ramp_weights = (col_freq + 0.5) / K
    coef_rows = coefficients.reshape(2 * columns, harmonics)
    harm_shift = (jnp.arange(harmonics, dtype=jnp.int32) - harmonics // 2).astype(jnp.float32)
    norm_scale = 1.0 / math.sqrt(harmonics)
    phase_tab = angles[:, None] * harm_shift[None, :]
    tabs = jnp.concatenate(
        [jnp.cos(phase_tab) * norm_scale, jnp.sin(phase_tab) * norm_scale]
    )

    def to_image(coef):
        prod = lax.dot_general(
            tabs, coef, (((1,), (1,)), ((), ())), precision=highest
        )
        cos_part, sin_part = prod[:total_angles], prod[total_angles:]
        real = cos_part[:, :columns] - sin_part[:, columns:]
        imag = cos_part[:, columns:] + sin_part[:, :columns]
        return real, imag

    model_real, model_imag = to_image(coef_rows)
    diff_real = model_real - filt_real
    diff_imag = model_imag - filt_imag
    resid_real = ramp_weights * diff_real
    resid_imag = ramp_weights * diff_imag
    energy = (diff_real * resid_real + diff_imag * resid_imag).reshape(
        total_angles, ROWS, block_freqs
    )
    misfit_table = jnp.sum(energy, axis=2) / K
    stacked = jnp.concatenate(
        [
            jnp.concatenate([resid_real, resid_imag], axis=1),
            jnp.concatenate([resid_imag, -resid_real], axis=1),
        ]
    )
    gram = lax.dot_general(tabs, tabs, (((1,), (1,)), ((), ())), precision=highest)
    gram_real = gram[:total_angles, :total_angles] + gram[total_angles:, total_angles:]
    gram_imag = gram[total_angles:, :total_angles] - gram[:total_angles, total_angles:]
    gram_both = jnp.concatenate(
        [
            jnp.concatenate([gram_real, -gram_imag], axis=1),
            jnp.concatenate([gram_imag, gram_real], axis=1),
        ]
    )
    resid_both = jnp.concatenate([resid_real, resid_imag])
    image_both = jnp.dot(gram_both, resid_both, precision=lax.Precision.HIGH)
    image_real, image_imag = image_both[:total_angles], image_both[total_angles:]
    owners = ang_count * sl_count
    if per_dev == 2 and sl_count == 2:
        cells = jnp.concatenate(
            [
                diff_real * resid_real + diff_imag * resid_imag,
                resid_real * image_real + resid_imag * image_imag,
                ramp_weights * (image_real * image_real + image_imag * image_imag),
            ],
            axis=1,
        )
        cell_ids = jnp.arange(3 * columns, dtype=jnp.int32)
        out_ids = jnp.arange(ROWS + 2, dtype=jnp.int32)
        target = jnp.where(
            cell_ids < columns, cell_ids // block_freqs, ROWS + cell_ids // columns - 1
        )
        scale = jnp.where(cell_ids < columns, 1.0 / K, 1.0).astype(jnp.float32)
        summing = jnp.where(target[:, None] == out_ids[None, :], scale[:, None], 0.0)
        sums = jnp.dot(cells, summing, precision=highest)
        table = sums[:, :ROWS]
        row_ids = jnp.arange(owners, dtype=jnp.int32)
        lane_ids = jnp.arange(ROWS, dtype=jnp.int32)
        row_swap = ((row_ids[:, None] ^ 1) == row_ids[None, :]).astype(jnp.float32)
        lane_swap = ((lane_ids[:, None] ^ rows_dev) == lane_ids[None, :]).astype(jnp.float32)
        swapped = jnp.dot(
            row_swap, jnp.dot(table, lane_swap, precision=highest), precision=highest
        )
        same_half = (row_ids[:, None] % 2) == ((lane_ids[None, :] // rows_dev) % 2)
        by_owner = jnp.where(same_half, table, swapped)
        spread = jnp.ones((owners, total_angles), jnp.float32)
        scalars = jnp.dot(spread, sums[:, ROWS:], precision=highest)
    else:
        curvature = jnp.sum(ramp_weights * (image_real * image_real + image_imag * image_imag))
        grad_norm = jnp.sum(resid_real * image_real + resid_imag * image_imag)
        by_owner = misfit_table.reshape(ang_count, per_dev, sl_count, rows_dev)
        by_owner = jnp.swapaxes(by_owner, 1, 2).reshape(owners, per_dev * rows_dev)
        scalars = jnp.broadcast_to(jnp.stack([grad_norm, curvature])[None], (owners, 2))
    payload = jnp.concatenate([by_owner, scalars], axis=1)
    received = lax.all_to_all(payload, ANG_SL, 0, 0, tiled=True)
    totals = jnp.sum(received, axis=0)
    misfit = totals[: per_dev * rows_dev].reshape(per_dev, rows_dev)
    step_size = totals[per_dev * rows_dev] / (totals[per_dev * rows_dev + 1] + small_eps)
    step_grad = lax.dot_general(
        -step_size * stacked, tabs, (((0,), (0,)), ((), ())), precision=lax.Precision.HIGH
    )
    updated = coefficients + step_grad.reshape(coefficients.shape)
    return (updated, misfit)


def solution(mesh):
    torus = Mesh(
        mesh.devices.reshape(8, 2, 4, 2, mesh.shape["sl"]),
        ("ang_0", "ang_1", "ang_2", "ang_3", "sl"),
    )
    in_specs = (P(ANG, "sl", None), P(), P(ANG), P(), P(None, None, ANG_SL, None))
    out_specs = (P(None, None, ANG_SL, None), P(ANG, "sl"))
    return jax.shard_map(
        step_body, mesh=torus, in_specs=in_specs, out_specs=out_specs, check_vma=False
    )
```
